512 devices in a mesh: section: 2 (over z_lo), tensor: 4 (over x), seq: 64 (over y, z_hi, core).
Axes of the slice: x: 4, y: 8, z: 8 (z_hi: 4, z_lo: 2; z = z_hi * 2 + z_lo), core: 2. Of those that a mesh axis runs over, the one named last changes fastest.
Arguments:
- tokens: bfloat16 [16384, 2560], P('seq', ('section', 'tensor')), may hold values from -6 to 6
- w_query: bfloat16 [2560, 2048], P(None, ('section', 'tensor')), may hold values from -0.125 to 0.125
- w_keyval: bfloat16 [2560, 2048], P(None, ('section', 'tensor')), may hold values from -0.125 to 0.125
- w_out: bfloat16 [2048, 2560], P(('section', 'tensor')), may hold values from -0.125 to 0.125
- w_gateup: bfloat16 [2560, 2, 5120], P('seq', None, ('section', 'tensor')), may hold values from -0.125 to 0.125
- attn_gain: float32 [2560], replicated, may hold values from 0.1 to 1.9
- post_gain: float32 [2560], replicated, may hold values from 0.1 to 1.9
- mlp_gain: float32 [2560], replicated, may hold values from 0.1 to 1.9
- query_gain: float32 [256], replicated, may hold values from 0.7 to 6.5
- key_gain: float32 [256], replicated, may hold values from 0.7 to 6.5
- prompt_lengths: int32 [8], replicated, may hold values from 1 to 4096, as said below
- page_slots: int32 [128], P('seq'), may hold values from 0 to 1, as said below
Outputs:
- hidden: bfloat16 [16384, 5120], P('seq', ('section', 'tensor'))
- page_cache: bfloat16 [128, 128, 2048], P('seq', None, ('section', 'tensor'))
The draws below stay inside these ranges and needn't reach their ends.
Inputs may be any that keep to these rules, and one draw needn't show every extreme that they name: `prompt_lengths`: each prompt has at least one token; they sum to 16384; one prompt has exactly 4096 tokens and begins strictly inside a token block. `page_slots`: within each aligned group of 2 pages (the pages of one token block) the slots are a permutation of 0 to 1.
All inputs are finite; a program needn't handle non-finite values.
Results may differ from the reference program's by a relative error of at most 0.01.
The reference program's roundings to bfloat16 on the way count: a program that leaves them out, or rounds other values in their place, can miss the bound.
Values may be sent and summed in bfloat16 or wider, within the bound.
No kernel may reach another device: no remote copies, remote signals or barrier semaphores. Data moves between devices by JAX's collectives and lax.ppermute only.
A program may use at most 64 MiB of HBM per device.

```python
import jax
import jax.numpy as jnp
from jax import lax

D = 2560
HD = 256
QH = 8
KVH = 4
FF = 5120
PAGE = 128
TOK_DEV = 256
TOKENS = 16384
SPAN = 16
LMAX = 4096
PROMPTS = 8
PAGES = 128
PAGES_DEV = 2
N_SEQ = 64


def draw_query_gain(key, part):
    return jax.random.uniform(key, (HD,), jnp.float32, 0.7, 1.6)


def draw_key_gain(key, part):
    mixed_key = jax.random.fold_in(key, 7)
    return jax.random.uniform(mixed_key, (HD,), jnp.float32, 0.7, 1.6)


def split_total(split_key, total, count):
    weights = jax.random.randint(split_key, (count,), 1, 17).astype(jnp.int32)
    spare = (total - count).astype(jnp.int32)
    extra = spare * weights // jnp.sum(weights)
    extra = jnp.minimum(extra, LMAX - 1).astype(jnp.int32)
    leftover = spare - jnp.sum(extra)
    for number in range(count):
        added = jnp.minimum(LMAX - 1 - extra[number], leftover)
        extra = extra.at[number].add(added)
        leftover = leftover - added
    return (extra + 1).astype(jnp.int32)


def draw_prompt_lengths(key, part):
    blocks = TOKENS // TOK_DEV
    middle = blocks // 2
    offset = jax.random.randint(jax.random.fold_in(key, 3), (), TOK_DEV // 4, 3 * TOK_DEV // 4 + 1).astype(jnp.int32)
    before_count = (middle - SPAN) * TOK_DEV // LMAX + 1
    after_count = PROMPTS - 1 - before_count
    before_total = (middle - SPAN) * TOK_DEV + offset
    after_total = TOKENS - LMAX - before_total
    before = split_total(jax.random.fold_in(key, 5), before_total, before_count)
    after = split_total(jax.random.fold_in(key, 9), after_total, after_count)
    return jnp.concatenate([before, jnp.full((1,), LMAX, jnp.int32), after]).astype(jnp.int32)


def draw_page_slots(key, part):
    groups = PAGES // PAGES_DEV
    group_keys = jax.random.split(jax.random.fold_in(key, 11), groups)
    table = jax.vmap(lambda single_key: jax.random.permutation(single_key, PAGES_DEV))(group_keys)
    return table.reshape(PAGES).astype(jnp.int32)


def block_scale(own_key, dims, pieces, smallest, high):
    def one(axis_at, blocks):
        steps = jax.random.uniform(jax.random.fold_in(jax.random.fold_in(own_key, 6), axis_at), (blocks,), jnp.float32, smallest / len(pieces), high / len(pieces))
        return jnp.repeat(jnp.exp(steps), dims[axis_at] // blocks).reshape((-1,) + (1,) * (len(dims) - axis_at - 1))

    gain = one(*pieces[0])
    for cut in pieces[1:]:
        gain = gain * one(*cut)
    return gain


def bell_draw(own_key, dims, spread, reach, cuts=(), kind=jnp.bfloat16):
    gain = block_scale(own_key, dims, cuts, -0.22, 0.18) if cuts else 1.0
    entries = jax.random.normal(own_key, dims, jnp.float32) * spread * gain
    return jnp.minimum(jnp.maximum(entries, -reach), reach).astype(kind)


def setup_inputs(seed: int = 0) -> dict:
    key_list = jax.random.split(jax.random.key(seed), 13)
    tokens = bell_draw(key_list[0], (TOKENS, D), 1.0, 6.0, ((0, 64), (1, 8)))
    w_query = bell_draw(key_list[1], (D, QH * HD), D ** -0.5, 0.125, ((1, 8),))
    w_keyval = bell_draw(key_list[2], (D, KVH * 2 * HD), D ** -0.5, 0.125, ((1, 8),))
    w_out = bell_draw(key_list[3], (QH * HD, D), (QH * HD) ** -0.5, 0.125, ((0, 8),))
    w_gateup = bell_draw(key_list[4], (D, 2, FF), D ** -0.5, 0.125, ((0, 64), (2, 8)))
    attn_gain = jnp.clip(1.0 + 0.18 * jax.random.normal(key_list[5], (D,), jnp.float32), 0.1, 1.9)
    post_gain = jnp.clip(1.0 + 0.18 * jax.random.normal(key_list[6], (D,), jnp.float32), 0.1, 1.9)
    mlp_gain = jnp.clip(1.0 + 0.18 * jax.random.normal(key_list[7], (D,), jnp.float32), 0.1, 1.9)
    query_gain = draw_query_gain(jax.random.fold_in(key_list[12], 71), 0)
    key_gain = draw_key_gain(jax.random.fold_in(key_list[12], 71), 0)
    prompt_lengths = draw_prompt_lengths(jax.random.fold_in(key_list[12], 71), 0)
    page_slots = draw_page_slots(jax.random.fold_in(key_list[12], 71), 0)
    return {"tokens": tokens, "w_query": w_query, "w_keyval": w_keyval, "w_out": w_out, "w_gateup": w_gateup, "attn_gain": attn_gain, "post_gain": post_gain, "mlp_gain": mlp_gain, "query_gain": query_gain, "key_gain": key_gain, "prompt_lengths": prompt_lengths, "page_slots": page_slots}


NORM_EPS = 1e-06
ROPE_BASE = 1000000.0
ROPE_FACTOR = 8.0

def rms_norm(values, weights):
    values = values.astype(jnp.float32)
    inverse = lax.rsqrt(lax.optimization_barrier(jnp.mean(values * values, axis=-1, keepdims=True)) + NORM_EPS)
    return values * inverse * weights.astype(jnp.float32)

def angle_tables(position, head_width):
    halfway = head_width // 2
    exponent = jnp.arange(halfway, dtype=jnp.float32) * (2.0 / head_width)
    frequency = ROPE_BASE ** (-exponent)
    angles = (position.astype(jnp.float32) / ROPE_FACTOR)[:, None] * frequency[None, :]
    return (jnp.cos(angles), jnp.sin(angles))

def rotary(values, cosine_table, sine_table):
    halfway = values.shape[-1] // 2
    lower_half = values[..., :halfway]
    upper_half = values[..., halfway:]
    return jnp.concatenate([lower_half * cosine_table - upper_half * sine_table, upper_half * cosine_table + lower_half * sine_table], axis=-1)

def reference(tokens, w_query, w_keyval, w_out, w_gateup, attn_gain, post_gain, mlp_gain, query_gain, key_gain, prompt_lengths, page_slots):
    row_index = jnp.arange(TOKENS, dtype=jnp.int32)
    prompt_ends = jnp.cumsum(prompt_lengths).astype(jnp.int32)
    prompt_starts = prompt_ends - prompt_lengths
    segment = lax.optimization_barrier(jnp.sum((prompt_ends[None, :] <= row_index[:, None]).astype(jnp.int32), axis=1))
    position = row_index - jnp.take(prompt_starts, segment)
    normed = rms_norm(tokens, attn_gain).astype(jnp.bfloat16)
    projected = jnp.dot(normed, w_keyval, preferred_element_type=jnp.float32).astype(jnp.bfloat16)
    projected = projected.reshape(TOKENS, KVH, 2, 2, HD // 2)
    raw_keys = projected[:, :, :, 0, :].reshape(TOKENS, KVH, HD)
    values_all = projected[:, :, :, 1, :].reshape(TOKENS, KVH, HD)
    cosine_table, sine_table = angle_tables(position, HD)
    keys_all = rotary(rms_norm(raw_keys, key_gain), cosine_table[:, None, :], sine_table[:, None, :]).astype(jnp.bfloat16)
    stacked = jnp.stack([keys_all.reshape(TOKENS, KVH, 2, HD // 2), values_all.reshape(TOKENS, KVH, 2, HD // 2)], axis=3)
    page_rows = stacked.reshape(PAGES, PAGE, KVH * 2 * HD)
    target = jnp.arange(PAGES, dtype=jnp.int32) // PAGES_DEV * PAGES_DEV + page_slots
    page_cache = jnp.zeros_like(page_rows).at[target].set(page_rows)
    window = (SPAN + 1) * TOK_DEV
    padding = SPAN * TOK_DEV
    keys_pad = jnp.concatenate([jnp.zeros((padding, KVH, HD), jnp.bfloat16), keys_all], axis=0)
    values_pad = jnp.concatenate([jnp.zeros((padding, KVH, HD), jnp.bfloat16), values_all], axis=0)
    segment_pad = jnp.concatenate([jnp.full((padding,), -1, jnp.int32), segment])
    score_scale = HD ** (-0.5)
    group = QH // KVH

    def one_block(block_id):
        begin_row = (block_id * TOK_DEV).astype(jnp.int32)
        rows_in = lax.dynamic_slice_in_dim(normed, begin_row, TOK_DEV, 0)
        queries = jnp.dot(rows_in, w_query, preferred_element_type=jnp.float32).reshape(TOK_DEV, QH, HD)
        cosine_rows = lax.dynamic_slice_in_dim(cosine_table, begin_row, TOK_DEV, 0)
        sine_rows = lax.dynamic_slice_in_dim(sine_table, begin_row, TOK_DEV, 0)
        queries = rotary(rms_norm(queries, query_gain), cosine_rows[:, None, :], sine_rows[:, None, :]).astype(jnp.bfloat16)
        keys_window = lax.dynamic_slice_in_dim(keys_pad, begin_row, window, 0)
        values_window = lax.dynamic_slice_in_dim(values_pad, begin_row, window, 0)
        query_segment = lax.dynamic_slice_in_dim(segment, begin_row, TOK_DEV, 0)
        key_segment = lax.dynamic_slice_in_dim(segment_pad, begin_row, window, 0)
        query_index = begin_row + jnp.arange(TOK_DEV, dtype=jnp.int32)
        key_index = begin_row - padding + jnp.arange(window, dtype=jnp.int32)
        allowed = (key_segment[None, :] == query_segment[:, None]) & (key_index[None, :] <= query_index[:, None])
        expanded_keys = jnp.repeat(keys_window, group, axis=1).astype(jnp.float32)
        expanded_values = jnp.repeat(values_window, group, axis=1).astype(jnp.float32)
        scores = jnp.einsum('rhd,khd->hrk', queries.astype(jnp.float32), expanded_keys) * score_scale
        scores = jnp.where(allowed[None, :, :], scores, -jnp.inf)
        row_max = lax.optimization_barrier(jnp.max(scores, axis=-1, keepdims=True))
        exponent_terms = jnp.exp(scores - row_max)
        probs = (exponent_terms / lax.optimization_barrier(jnp.sum(exponent_terms, axis=-1, keepdims=True))).astype(jnp.bfloat16)
        attention_out = jnp.einsum('hrk,khd->rhd', probs.astype(jnp.float32), expanded_values).astype(jnp.bfloat16)
        attended = jnp.dot(attention_out.reshape(TOK_DEV, QH * HD), w_out, preferred_element_type=jnp.float32)
        token_rows = lax.dynamic_slice_in_dim(tokens, begin_row, TOK_DEV, 0).astype(jnp.float32)
        residual = token_rows + rms_norm(attended, post_gain)
        ffn_input = rms_norm(residual, mlp_gain).astype(jnp.bfloat16)
        gate_part = jnp.dot(ffn_input, w_gateup[:, 0, :], preferred_element_type=jnp.float32)
        up_part = jnp.dot(ffn_input, w_gateup[:, 1, :], preferred_element_type=jnp.float32)
        return (jax.nn.gelu(gate_part, approximate=True) * up_part).astype(jnp.bfloat16)
    hidden = lax.map(one_block, jnp.arange(N_SEQ, dtype=jnp.int32)).reshape(TOKENS, FF)
    return (hidden, page_cache)
```

```python
import jax
import jax.numpy as jnp
from jax import lax
from jax.sharding import PartitionSpec as P

REACH = 16


NORM_EPS = 1e-06
ROPE_BASE = 1000000.0
ROPE_FACTOR = 8.0


def swapped(value, axis, bit):
    mask = 2**bit
    pairs = [(source, source ^ mask) for source in range(lax.axis_size(axis))]
    return lax.ppermute(value, axis, pairs)


def shifted(block, axis, distance):
    devices = range(lax.axis_size(axis))
    route = [(i - distance, i) for i in devices if i - distance in devices]
    return lax.ppermute(block, axis, route)


GROUP = ("section", "tensor")


def group_exchange(value, k):
    count = lax.axis_size("section") * lax.axis_size("tensor")
    return lax.ppermute(value, GROUP, [(g, g ^ k) for g in range(count)])


def group_parts(value):
    count = lax.axis_size("section") * lax.axis_size("tensor")
    me = lax.axis_index(GROUP)
    parts = jnp.stack([value] + [group_exchange(value, k) for k in range(1, count)])
    return jnp.take(parts, me ^ jnp.arange(count, dtype=jnp.int32), axis=0)


def group_gather(block):
    rows, width = block.shape
    parts = group_parts(block)
    return parts.transpose(1, 0, 2).reshape(rows, parts.shape[0] * width)


def group_sum(vector):
    return jnp.sum(group_parts(vector), axis=0)


def group_reduce_scatter(partial):
    count = lax.axis_size("section") * lax.axis_size("tensor")
    me = lax.axis_index(GROUP)
    rows, total = partial.shape
    blocks = partial.reshape(rows, count, total // count)
    result = lax.dynamic_index_in_dim(blocks, me, axis=1, keepdims=False)
    for k in range(1, count):
        send = lax.dynamic_index_in_dim(blocks, me ^ k, axis=1, keepdims=False)
        result = result + group_exchange(send, k)
    return result


def rms_norm(values, weights):
    values = values.astype(jnp.float32)
    inverse = lax.rsqrt(jnp.mean(values * values, axis=-1, keepdims=True) + NORM_EPS)
    return values * inverse * weights


def angle_tables(position, head_width):
    halfway = head_width // 2
    exponent = jnp.arange(halfway, dtype=jnp.float32) * (2.0 / head_width)
    frequency = ROPE_BASE ** (-exponent)
    angles = (position.astype(jnp.float32) / ROPE_FACTOR)[:, None] * frequency[None, :]
    return (jnp.cos(angles), jnp.sin(angles))


def rotary(values, cosine_table, sine_table):
    halfway = values.shape[-1] // 2
    lower_half = values[..., :halfway]
    upper_half = values[..., halfway:]
    return jnp.concatenate(
        [
            lower_half * cosine_table - upper_half * sine_table,
            upper_half * cosine_table + lower_half * sine_table,
        ],
        axis=-1,
    )


def local(
    tokens,
    w_query,
    w_keyval,
    w_out,
    w_gateup,
    attn_gain,
    post_gain,
    mlp_gain,
    query_gain,
    key_gain,
    prompt_lengths,
    page_slots,
):
    row_count = tokens.shape[0]
    head_width = w_query.shape[1]
    halfway = head_width // 2
    unit_count = w_gateup.shape[2]
    span_blocks = min(REACH, lax.axis_size("seq") // 2)
    features = group_gather(tokens)
    first_row = lax.axis_index("seq") * row_count
    prompt_ends = jnp.cumsum(prompt_lengths)
    prompt_starts = prompt_ends - prompt_lengths
    query_index = first_row + jnp.arange(row_count, dtype=jnp.int32)
    query_segment = jnp.sum(
        (prompt_ends[None, :] <= query_index[:, None]).astype(jnp.int32), axis=1
    )
    chosen = query_segment[:, None] == jnp.arange(prompt_ends.shape[0], dtype=jnp.int32)[None, :]
    query_position = query_index - jnp.sum(jnp.where(chosen, prompt_starts[None, :], 0), axis=1)
    cosine_table, sine_table = angle_tables(query_position, head_width)
    normed = rms_norm(features, attn_gain).astype(jnp.bfloat16)
    queries = jnp.dot(normed, w_query, preferred_element_type=jnp.float32)
    queries = rotary(rms_norm(queries, query_gain), cosine_table, sine_table).astype(jnp.bfloat16)
    own_half = jnp.dot(normed, w_keyval, preferred_element_type=jnp.float32).astype(jnp.bfloat16)
    other_half = swapped(own_half, "tensor", 0)
    is_lower = lax.axis_index("tensor") % 2 == 0
    lower_part = jnp.where(is_lower, own_half, other_half)
    upper_part = jnp.where(is_lower, other_half, own_half)
    raw_keys = jnp.concatenate([lower_part[:, :halfway], upper_part[:, :halfway]], axis=1)
    values_full = jnp.concatenate([lower_part[:, halfway:], upper_part[:, halfway:]], axis=1)
    keys_full = rotary(rms_norm(raw_keys, key_gain), cosine_table, sine_table).astype(jnp.bfloat16)
    own_keys = jnp.where(is_lower, keys_full[:, :halfway], keys_full[:, halfway:])
    page_rows = jnp.concatenate([own_keys, own_half[:, halfway:]], axis=1)
    pages_here = page_slots.shape[0]
    page_rows = page_rows.reshape(pages_here, row_count // pages_here, head_width)
    page_cache = jnp.zeros_like(page_rows).at[page_slots].set(page_rows)
    key_block = jnp.stack([keys_full, values_full])
    received = [key_block]
    for distance in range(1, span_blocks + 1):
        received.append(shifted(key_block, "seq", distance))
    window_stack = jnp.stack(received)
    all_keys = window_stack[:, 0].reshape(-1, head_width)
    all_values = window_stack[:, 1].reshape(-1, head_width)
    offsets = (jnp.arange(span_blocks + 1, dtype=jnp.int32) * row_count)[:, None]
    key_index = (first_row - offsets + jnp.arange(row_count, dtype=jnp.int32)[None, :]).reshape(-1)
    key_segment = jnp.sum((prompt_ends[None, :] <= key_index[:, None]).astype(jnp.int32), axis=1)
    key_segment = jnp.where(key_index >= 0, key_segment, -1)
    allowed = (key_segment[None, :] == query_segment[:, None]) & (
        key_index[None, :] <= query_index[:, None]
    )
    scores = lax.dot_general(
        queries, all_keys, (((1,), (1,)), ((), ())), preferred_element_type=jnp.float32
    ) * head_width ** (-0.5)
    scores = jnp.where(allowed, scores, -jnp.inf)
    row_max = jnp.max(scores, axis=1, keepdims=True)
    exponent_terms = jnp.exp(scores - row_max)
    weights_low = (exponent_terms / jnp.sum(exponent_terms, axis=1, keepdims=True)).astype(
        jnp.bfloat16
    )
    attention_out = jnp.dot(weights_low, all_values, preferred_element_type=jnp.float32).astype(
        jnp.bfloat16
    )
    head_terms = jnp.dot(attention_out, w_out, preferred_element_type=jnp.float32)
    attended = group_reduce_scatter(head_terms)
    width = attended.shape[1]
    first_column = lax.axis_index(GROUP) * width
    post_local = lax.dynamic_slice_in_dim(post_gain, first_column, width)
    mlp_local = lax.dynamic_slice_in_dim(mlp_gain, first_column, width)
    model_width = features.shape[1]
    attended_inverse = lax.rsqrt(
        group_sum(jnp.sum(attended * attended, axis=1)) / model_width + NORM_EPS
    )
    residual = tokens.astype(jnp.float32) + attended * attended_inverse[:, None] * post_local
    residual_inverse = lax.rsqrt(
        group_sum(jnp.sum(residual * residual, axis=1)) / model_width + NORM_EPS
    )
    ffn_local = (residual * residual_inverse[:, None] * mlp_local).astype(jnp.bfloat16)
    ffn_input = group_gather(ffn_local)
    row_piece = lax.all_gather(w_gateup, "seq", axis=0, tiled=True)
    piece_rows = row_piece.shape[0]
    projected = jnp.dot(
        ffn_input, row_piece.reshape(piece_rows, 2 * unit_count), preferred_element_type=jnp.float32
    )
    hidden = (
        jax.nn.gelu(projected[:, :unit_count], approximate=True) * projected[:, unit_count:]
    ).astype(jnp.bfloat16)
    return (hidden, page_cache)


def solution(mesh):
    return jax.shard_map(
        local,
        mesh=mesh,
        in_specs=(
            P("seq", ("section", "tensor")),
            P(None, ("section", "tensor")),
            P(None, ("section", "tensor")),
            P(("section", "tensor"), None),
            P("seq", None, ("section", "tensor")),
            P(),
            P(),
            P(),
            P(),
            P(),
            P(),
            P("seq"),
        ),
        out_specs=(P("seq", ("section", "tensor")), P("seq", None, ("section", "tensor"))),
        check_vma=False,
    )
```

```python
import jax
import jax.numpy as jnp
from jax import lax
from jax.sharding import PartitionSpec as P

REACH = 16


NORM_EPS = 1e-06
ROPE_BASE = 1000000.0
ROPE_FACTOR = 8.0


def swapped(value, axis, bit):
    mask = 2**bit
    pairs = [(source, source ^ mask) for source in range(lax.axis_size(axis))]
    return lax.ppermute(value, axis, pairs)


def shifted(block, axis, distance):
    devices = range(lax.axis_size(axis))
    route = [(i - distance, i) for i in devices if i - distance in devices]
    return lax.ppermute(block, axis, route)


GROUP = ("section", "tensor")


def group_count():
    return lax.axis_size("section") * lax.axis_size("tensor")


def group_parts(value):
    spread = jnp.broadcast_to(value[None], (group_count(),) + value.shape)
    return lax.all_to_all(spread, GROUP, 0, 0, tiled=True)


def group_gather(block):
    rows, width = block.shape
    parts = group_parts(block)
    return parts.transpose(1, 0, 2).reshape(rows, parts.shape[0] * width)


def group_sum(vector):
    return jnp.sum(group_parts(vector), axis=0)


def group_reduce_scatter(partial):
    count = group_count()
    rows, total = partial.shape
    chunks = partial.reshape(rows, count, total // count).transpose(1, 0, 2)
    return jnp.sum(lax.all_to_all(chunks, GROUP, 0, 0, tiled=True), axis=0)


def rms_norm(values, weights):
    values = values.astype(jnp.float32)
    inverse = lax.rsqrt(jnp.mean(values * values, axis=-1, keepdims=True) + NORM_EPS)
    return values * inverse * weights


def angle_tables(position, head_width):
    halfway = head_width // 2
    exponent = jnp.arange(halfway, dtype=jnp.float32) * (2.0 / head_width)
    frequency = ROPE_BASE ** (-exponent)
    angles = (position.astype(jnp.float32) / ROPE_FACTOR)[:, None] * frequency[None, :]
    return (jnp.cos(angles), jnp.sin(angles))


def rotary(values, cosine_table, sine_table):
    halfway = values.shape[-1] // 2
    lower_half = values[..., :halfway]
    upper_half = values[..., halfway:]
    return jnp.concatenate(
        [
            lower_half * cosine_table - upper_half * sine_table,
            upper_half * cosine_table + lower_half * sine_table,
        ],
        axis=-1,
    )


def local(
    tokens,
    w_query,
    w_keyval,
    w_out,
    w_gateup,
    attn_gain,
    post_gain,
    mlp_gain,
    query_gain,
    key_gain,
    prompt_lengths,
    page_slots,
):
    row_count = tokens.shape[0]
    head_width = w_query.shape[1]
    halfway = head_width // 2
    unit_count = w_gateup.shape[2]
    span_blocks = min(REACH, lax.axis_size("seq") // 2)
    features = group_gather(tokens)
    first_row = lax.axis_index("seq") * row_count
    prompt_ends = jnp.cumsum(prompt_lengths)
    prompt_starts = prompt_ends - prompt_lengths
    query_index = first_row + jnp.arange(row_count, dtype=jnp.int32)
    query_segment = jnp.sum(
        (prompt_ends[None, :] <= query_index[:, None]).astype(jnp.int32), axis=1
    )
    chosen = query_segment[:, None] == jnp.arange(prompt_ends.shape[0], dtype=jnp.int32)[None, :]
    query_position = query_index - jnp.sum(jnp.where(chosen, prompt_starts[None, :], 0), axis=1)
    cosine_table, sine_table = angle_tables(query_position, head_width)
    normed = rms_norm(features, attn_gain).astype(jnp.bfloat16)
    queries = jnp.dot(normed, w_query, preferred_element_type=jnp.float32)
    queries = rotary(rms_norm(queries, query_gain), cosine_table, sine_table).astype(jnp.bfloat16)
    own_half = jnp.dot(normed, w_keyval, preferred_element_type=jnp.float32).astype(jnp.bfloat16)
    other_half = swapped(own_half, "tensor", 0)
    is_lower = lax.axis_index("tensor") % 2 == 0
    lower_part = jnp.where(is_lower, own_half, other_half)
    upper_part = jnp.where(is_lower, other_half, own_half)
    raw_keys = jnp.concatenate([lower_part[:, :halfway], upper_part[:, :halfway]], axis=1)
    values_full = jnp.concatenate([lower_part[:, halfway:], upper_part[:, halfway:]], axis=1)
    keys_full = rotary(rms_norm(raw_keys, key_gain), cosine_table, sine_table).astype(jnp.bfloat16)
    own_keys = jnp.where(is_lower, keys_full[:, :halfway], keys_full[:, halfway:])
    page_rows = jnp.concatenate([own_keys, own_half[:, halfway:]], axis=1)
    pages_here = page_slots.shape[0]
    page_rows = page_rows.reshape(pages_here, row_count // pages_here, head_width)
    page_cache = jnp.zeros_like(page_rows).at[page_slots].set(page_rows)
    key_block = jnp.stack([keys_full, values_full])
    received = [key_block]
    for distance in range(1, span_blocks + 1):
        received.append(shifted(key_block, "seq", distance))
    window_stack = jnp.stack(received)
    all_keys = window_stack[:, 0].reshape(-1, head_width)
    all_values = window_stack[:, 1].reshape(-1, head_width)
    offsets = (jnp.arange(span_blocks + 1, dtype=jnp.int32) * row_count)[:, None]
    key_index = (first_row - offsets + jnp.arange(row_count, dtype=jnp.int32)[None, :]).reshape(-1)
    key_segment = jnp.sum((prompt_ends[None, :] <= key_index[:, None]).astype(jnp.int32), axis=1)
    key_segment = jnp.where(key_index >= 0, key_segment, -1)
    allowed = (key_segment[None, :] == query_segment[:, None]) & (
        key_index[None, :] <= query_index[:, None]
    )
    scores = lax.dot_general(
        queries, all_keys, (((1,), (1,)), ((), ())), preferred_element_type=jnp.float32
    ) * head_width ** (-0.5)
    scores = jnp.where(allowed, scores, -jnp.inf)
    row_max = jnp.max(scores, axis=1, keepdims=True)
    exponent_terms = jnp.exp(scores - row_max)
    weights_low = (exponent_terms / jnp.sum(exponent_terms, axis=1, keepdims=True)).astype(
        jnp.bfloat16
    )
    attention_out = jnp.dot(weights_low, all_values, preferred_element_type=jnp.float32).astype(
        jnp.bfloat16
    )
    head_terms = jnp.dot(attention_out, w_out, preferred_element_type=jnp.float32)
    attended = group_reduce_scatter(head_terms)
    width = attended.shape[1]
    first_column = lax.axis_index(GROUP) * width
    post_local = lax.dynamic_slice_in_dim(post_gain, first_column, width)
    mlp_local = lax.dynamic_slice_in_dim(mlp_gain, first_column, width)
    model_width = features.shape[1]
    attended_inverse = lax.rsqrt(
        group_sum(jnp.sum(attended * attended, axis=1)) / model_width + NORM_EPS
    )
    residual = tokens.astype(jnp.float32) + attended * attended_inverse[:, None] * post_local
    residual_inverse = lax.rsqrt(
        group_sum(jnp.sum(residual * residual, axis=1)) / model_width + NORM_EPS
    )
    ffn_local = (residual * residual_inverse[:, None] * mlp_local).astype(jnp.bfloat16)
    ffn_input = group_gather(ffn_local)
    row_piece = lax.all_gather(w_gateup, "seq", axis=0, tiled=True)
    piece_rows = row_piece.shape[0]
    projected = jnp.dot(
        ffn_input, row_piece.reshape(piece_rows, 2 * unit_count), preferred_element_type=jnp.float32
    )
    hidden = (
        jax.nn.gelu(projected[:, :unit_count], approximate=True) * projected[:, unit_count:]
    ).astype(jnp.bfloat16)
    return (hidden, page_cache)


def solution(mesh):
    return jax.shard_map(
        local,
        mesh=mesh,
        in_specs=(
            P("seq", ("section", "tensor")),
            P(None, ("section", "tensor")),
            P(None, ("section", "tensor")),
            P(("section", "tensor"), None),
            P("seq", None, ("section", "tensor")),
            P(),
            P(),
            P(),
            P(),
            P(),
            P(),
            P("seq"),
        ),
        out_specs=(P("seq", ("section", "tensor")), P("seq", None, ("section", "tensor"))),
        check_vma=False,
    )
```

```python
import jax
import jax.numpy as jnp
from jax import lax
from jax.sharding import PartitionSpec as P

REACH = 16


NORM_EPS = 1e-06
ROPE_BASE = 1000000.0
ROPE_FACTOR = 8.0


def swapped(value, axis, bit):
    mask = 2**bit
    pairs = [(source, source ^ mask) for source in range(lax.axis_size(axis))]
    return lax.ppermute(value, axis, pairs)


def shifted(block, axis, distance):
    devices = range(lax.axis_size(axis))
    route = [(i - distance, i) for i in devices if i - distance in devices]
    return lax.ppermute(block, axis, route)


GROUP = ("section", "tensor")


def group_count():
    return lax.axis_size("section") * lax.axis_size("tensor")


def group_parts(value):
    spread = jnp.broadcast_to(value[None], (group_count(),) + value.shape)
    return lax.all_to_all(spread, GROUP, 0, 0, tiled=True)


def group_gather(block):
    rows, width = block.shape
    parts = group_parts(block)
    return parts.transpose(1, 0, 2).reshape(rows, parts.shape[0] * width)


def group_sum(vector):
    return jnp.sum(group_parts(vector), axis=0)


def group_reduce_scatter(partial):
    count = group_count()
    rows, total = partial.shape
    chunks = partial.reshape(rows, count, total // count).transpose(1, 0, 2)
    return jnp.sum(lax.all_to_all(chunks, GROUP, 0, 0, tiled=True), axis=0)


def rms_norm(values, weights):
    values = values.astype(jnp.float32)
    inverse = lax.rsqrt(jnp.mean(values * values, axis=-1, keepdims=True) + NORM_EPS)
    return values * inverse * weights


def angle_tables(position, head_width):
    halfway = head_width // 2
    exponent = jnp.arange(halfway, dtype=jnp.float32) * (2.0 / head_width)
    frequency = ROPE_BASE ** (-exponent)
    angles = (position.astype(jnp.float32) / ROPE_FACTOR)[:, None] * frequency[None, :]
    return (jnp.cos(angles), jnp.sin(angles))


def rotary(values, cosine_table, sine_table):
    halfway = values.shape[-1] // 2
    lower_half = values[..., :halfway]
    upper_half = values[..., halfway:]
    return jnp.concatenate(
        [
            lower_half * cosine_table - upper_half * sine_table,
            upper_half * cosine_table + lower_half * sine_table,
        ],
        axis=-1,
    )


def local(
    tokens,
    w_query,
    w_keyval,
    w_out,
    w_gateup,
    attn_gain,
    post_gain,
    mlp_gain,
    query_gain,
    key_gain,
    prompt_lengths,
    page_slots,
):
    row_count = tokens.shape[0]
    head_width = w_query.shape[1]
    halfway = head_width // 2
    unit_count = w_gateup.shape[2]
    span_blocks = min(REACH, lax.axis_size("seq") // 2)
    features = group_gather(tokens)
    first_row = lax.axis_index("seq") * row_count
    prompt_ends = jnp.cumsum(prompt_lengths)
    prompt_starts = prompt_ends - prompt_lengths
    query_index = first_row + jnp.arange(row_count, dtype=jnp.int32)
    query_segment = jnp.sum(
        (prompt_ends[None, :] <= query_index[:, None]).astype(jnp.int32), axis=1
    )
    chosen = query_segment[:, None] == jnp.arange(prompt_ends.shape[0], dtype=jnp.int32)[None, :]
    query_position = query_index - jnp.sum(jnp.where(chosen, prompt_starts[None, :], 0), axis=1)
    cosine_table, sine_table = angle_tables(query_position, head_width)
    normed = rms_norm(features, attn_gain).astype(jnp.bfloat16)
    queries = jnp.dot(normed, w_query, preferred_element_type=jnp.float32)
    queries = rotary(rms_norm(queries, query_gain), cosine_table, sine_table).astype(jnp.bfloat16)
    own_half = jnp.dot(normed, w_keyval, preferred_element_type=jnp.float32).astype(jnp.bfloat16)
    other_half = swapped(own_half, "tensor", 0)
    is_lower = lax.axis_index("tensor") % 2 == 0
    lower_part = jnp.where(is_lower, own_half, other_half)
    upper_part = jnp.where(is_lower, other_half, own_half)
    raw_keys = jnp.concatenate([lower_part[:, :halfway], upper_part[:, :halfway]], axis=1)
    values_full = jnp.concatenate([lower_part[:, halfway:], upper_part[:, halfway:]], axis=1)
    keys_full = rotary(rms_norm(raw_keys, key_gain), cosine_table, sine_table).astype(jnp.bfloat16)
    own_keys = jnp.where(is_lower, keys_full[:, :halfway], keys_full[:, halfway:])
    page_rows = jnp.concatenate([own_keys, own_half[:, halfway:]], axis=1)
    pages_here = page_slots.shape[0]
    page_rows = page_rows.reshape(pages_here, row_count // pages_here, head_width)
    page_cache = jnp.zeros_like(page_rows).at[page_slots].set(page_rows)
    key_block = jnp.stack([keys_full, values_full])
    half_span = span_blocks // 2
    series = key_block[None]
    while series.shape[0] < half_span:
        series = jnp.concatenate([series, shifted(series, "seq", 2 * series.shape[0])], axis=0)
    series = jnp.concatenate([series, shifted(key_block, "seq", 2 * half_span)[None]], axis=0)
    partner = swapped(series, "seq", 0)
    parity = lax.axis_index("seq") % 2
    odd = lax.dynamic_slice_in_dim(partner, 1 - parity, half_span, axis=0)
    window_stack = jnp.concatenate([series, odd], axis=0)
    all_keys = window_stack[:, 0].reshape(-1, head_width)
    all_values = window_stack[:, 1].reshape(-1, head_width)
    distances = list(range(0, 2 * half_span + 1, 2)) + list(range(1, 2 * half_span, 2))
    offsets = (jnp.array(distances, dtype=jnp.int32) * row_count)[:, None]
    key_index = (first_row - offsets + jnp.arange(row_count, dtype=jnp.int32)[None, :]).reshape(-1)
    key_segment = jnp.sum((prompt_ends[None, :] <= key_index[:, None]).astype(jnp.int32), axis=1)
    key_segment = jnp.where(key_index >= 0, key_segment, -1)
    allowed = (key_segment[None, :] == query_segment[:, None]) & (
        key_index[None, :] <= query_index[:, None]
    )
    scores = lax.dot_general(
        queries, all_keys, (((1,), (1,)), ((), ())), preferred_element_type=jnp.float32
    ) * head_width ** (-0.5)
    scores = jnp.where(allowed, scores, -jnp.inf)
    row_max = jnp.max(scores, axis=1, keepdims=True)
    exponent_terms = jnp.exp(scores - row_max)
    weights_low = (exponent_terms / jnp.sum(exponent_terms, axis=1, keepdims=True)).astype(
        jnp.bfloat16
    )
    attention_out = jnp.dot(weights_low, all_values, preferred_element_type=jnp.float32).astype(
        jnp.bfloat16
    )
    head_terms = jnp.dot(attention_out, w_out, preferred_element_type=jnp.float32)
    attended = group_reduce_scatter(head_terms)
    width = attended.shape[1]
    first_column = lax.axis_index(GROUP) * width
    post_local = lax.dynamic_slice_in_dim(post_gain, first_column, width)
    mlp_local = lax.dynamic_slice_in_dim(mlp_gain, first_column, width)
    model_width = features.shape[1]
    attended_inverse = lax.rsqrt(
        group_sum(jnp.sum(attended * attended, axis=1)) / model_width + NORM_EPS
    )
    residual = tokens.astype(jnp.float32) + attended * attended_inverse[:, None] * post_local
    residual_inverse = lax.rsqrt(
        group_sum(jnp.sum(residual * residual, axis=1)) / model_width + NORM_EPS
    )
    ffn_local = (residual * residual_inverse[:, None] * mlp_local).astype(jnp.bfloat16)
    ffn_input = group_gather(ffn_local)
    row_piece = lax.all_gather(w_gateup, "seq", axis=0, tiled=True)
    piece_rows = row_piece.shape[0]
    projected = jnp.dot(
        ffn_input, row_piece.reshape(piece_rows, 2 * unit_count), preferred_element_type=jnp.float32
    )
    hidden = (
        jax.nn.gelu(projected[:, :unit_count], approximate=True) * projected[:, unit_count:]
    ).astype(jnp.bfloat16)
    return (hidden, page_cache)


def solution(mesh):
    return jax.shard_map(
        local,
        mesh=mesh,
        in_specs=(
            P("seq", ("section", "tensor")),
            P(None, ("section", "tensor")),
            P(None, ("section", "tensor")),
            P(("section", "tensor"), None),
            P("seq", None, ("section", "tensor")),
            P(),
            P(),
            P(),
            P(),
            P(),
            P(),
            P("seq"),
        ),
        out_specs=(P("seq", ("section", "tensor")), P("seq", None, ("section", "tensor"))),
        check_vma=False,
    )
```

```python
import jax
import jax.numpy as jnp
from jax import lax
from jax.sharding import PartitionSpec as P

REACH = 16


NORM_EPS = 1e-06
ROPE_BASE = 1000000.0
ROPE_FACTOR = 8.0


def swapped(value, axis, bit):
    mask = 2**bit
    pairs = [(source, source ^ mask) for source in range(lax.axis_size(axis))]
    return lax.ppermute(value, axis, pairs)


def shifted(block, axis, distance):
    devices = range(lax.axis_size(axis))
    route = [(i - distance, i) for i in devices if i - distance in devices]
    return lax.ppermute(block, axis, route)


GROUP = ("section", "tensor")


def group_count():
    return lax.axis_size("section") * lax.axis_size("tensor")


def group_parts(value):
    spread = jnp.broadcast_to(value[None], (group_count(),) + value.shape)
    return lax.all_to_all(spread, GROUP, 0, 0, tiled=True)


def group_gather(block):
    rows, width = block.shape
    parts = group_parts(block)
    return parts.transpose(1, 0, 2).reshape(rows, parts.shape[0] * width)


def group_sum(vector):
    return jnp.sum(group_parts(vector), axis=0)


def rms_norm(values, weights):
    values = values.astype(jnp.float32)
    inverse = lax.rsqrt(jnp.mean(values * values, axis=-1, keepdims=True) + NORM_EPS)
    return values * inverse * weights


def angle_tables(position, head_width):
    halfway = head_width // 2
    exponent = jnp.arange(halfway, dtype=jnp.float32) * (2.0 / head_width)
    frequency = ROPE_BASE ** (-exponent)
    angles = (position.astype(jnp.float32) / ROPE_FACTOR)[:, None] * frequency[None, :]
    return (jnp.cos(angles), jnp.sin(angles))


def rotary(values, cosine_table, sine_table):
    halfway = values.shape[-1] // 2
    lower_half = values[..., :halfway]
    upper_half = values[..., halfway:]
    return jnp.concatenate(
        [
            lower_half * cosine_table - upper_half * sine_table,
            upper_half * cosine_table + lower_half * sine_table,
        ],
        axis=-1,
    )


def local(
    tokens,
    w_query,
    w_keyval,
    w_out,
    w_gateup,
    attn_gain,
    post_gain,
    mlp_gain,
    query_gain,
    key_gain,
    prompt_lengths,
    page_slots,
):
    row_count = tokens.shape[0]
    head_width = w_query.shape[1]
    halfway = head_width // 2
    unit_count = w_gateup.shape[2]
    span_blocks = min(REACH, lax.axis_size("seq") // 2)
    features = group_gather(tokens)
    out_columns = lax.all_to_all(w_out, GROUP, 1, 0, tiled=True)
    first_row = lax.axis_index("seq") * row_count
    prompt_ends = jnp.cumsum(prompt_lengths)
    prompt_starts = prompt_ends - prompt_lengths
    query_index = first_row + jnp.arange(row_count, dtype=jnp.int32)
    query_segment = jnp.sum(
        (prompt_ends[None, :] <= query_index[:, None]).astype(jnp.int32), axis=1
    )
    chosen = query_segment[:, None] == jnp.arange(prompt_ends.shape[0], dtype=jnp.int32)[None, :]
    query_position = query_index - jnp.sum(jnp.where(chosen, prompt_starts[None, :], 0), axis=1)
    cosine_table, sine_table = angle_tables(query_position, head_width)
    normed = rms_norm(features, attn_gain).astype(jnp.bfloat16)
    queries = jnp.dot(normed, w_query, preferred_element_type=jnp.float32)
    queries = rotary(rms_norm(queries, query_gain), cosine_table, sine_table).astype(jnp.bfloat16)
    own_half = jnp.dot(normed, w_keyval, preferred_element_type=jnp.float32).astype(jnp.bfloat16)
    other_half = swapped(own_half, "tensor", 0)
    is_lower = lax.axis_index("tensor") % 2 == 0
    lower_part = jnp.where(is_lower, own_half, other_half)
    upper_part = jnp.where(is_lower, other_half, own_half)
    raw_keys = jnp.concatenate([lower_part[:, :halfway], upper_part[:, :halfway]], axis=1)
    values_full = jnp.concatenate([lower_part[:, halfway:], upper_part[:, halfway:]], axis=1)
    keys_full = rotary(rms_norm(raw_keys, key_gain), cosine_table, sine_table).astype(jnp.bfloat16)
    own_keys = jnp.where(is_lower, keys_full[:, :halfway], keys_full[:, halfway:])
    page_rows = jnp.concatenate([own_keys, own_half[:, halfway:]], axis=1)
    pages_here = page_slots.shape[0]
    page_rows = page_rows.reshape(pages_here, row_count // pages_here, head_width)
    page_cache = jnp.zeros_like(page_rows).at[page_slots].set(page_rows)
    key_block = jnp.stack([keys_full, values_full])
    half_span = span_blocks // 2
    series = key_block[None]
    while series.shape[0] < half_span:
        series = jnp.concatenate([series, shifted(series, "seq", 2 * series.shape[0])], axis=0)
    series = jnp.concatenate([series, shifted(key_block, "seq", 2 * half_span)[None]], axis=0)
    partner = swapped(series, "seq", 0)
    parity = lax.axis_index("seq") % 2
    odd = lax.dynamic_slice_in_dim(partner, 1 - parity, half_span, axis=0)
    window_stack = jnp.concatenate([series, odd], axis=0)
    all_keys = window_stack[:, 0].reshape(-1, head_width)
    all_values = window_stack[:, 1].reshape(-1, head_width)
    distances = list(range(0, 2 * half_span + 1, 2)) + list(range(1, 2 * half_span, 2))
    offsets = (jnp.array(distances, dtype=jnp.int32) * row_count)[:, None]
    key_index = (first_row - offsets + jnp.arange(row_count, dtype=jnp.int32)[None, :]).reshape(-1)
    key_segment = jnp.sum((prompt_ends[None, :] <= key_index[:, None]).astype(jnp.int32), axis=1)
    key_segment = jnp.where(key_index >= 0, key_segment, -1)
    allowed = (key_segment[None, :] == query_segment[:, None]) & (
        key_index[None, :] <= query_index[:, None]
    )
    scores = lax.dot_general(
        queries, all_keys, (((1,), (1,)), ((), ())), preferred_element_type=jnp.float32
    ) * head_width ** (-0.5)
    scores = jnp.where(allowed, scores, -jnp.inf)
    row_max = jnp.max(scores, axis=1, keepdims=True)
    exponent_terms = jnp.exp(scores - row_max)
    weights_low = (exponent_terms / jnp.sum(exponent_terms, axis=1, keepdims=True)).astype(
        jnp.bfloat16
    )
    attention_out = jnp.dot(weights_low, all_values, preferred_element_type=jnp.float32).astype(
        jnp.bfloat16
    )
    all_heads = group_gather(attention_out)
    attended = jnp.dot(all_heads, out_columns, preferred_element_type=jnp.float32)
    width = attended.shape[1]
    first_column = lax.axis_index(GROUP) * width
    post_local = lax.dynamic_slice_in_dim(post_gain, first_column, width)
    mlp_local = lax.dynamic_slice_in_dim(mlp_gain, first_column, width)
    model_width = features.shape[1]
    attended_inverse = lax.rsqrt(
        group_sum(jnp.sum(attended * attended, axis=1)) / model_width + NORM_EPS
    )
    residual = tokens.astype(jnp.float32) + attended * attended_inverse[:, None] * post_local
    residual_inverse = lax.rsqrt(
        group_sum(jnp.sum(residual * residual, axis=1)) / model_width + NORM_EPS
    )
    ffn_local = (residual * residual_inverse[:, None] * mlp_local).astype(jnp.bfloat16)
    ffn_input = group_gather(ffn_local)
    row_piece = lax.all_gather(w_gateup, "seq", axis=0, tiled=True)
    piece_rows = row_piece.shape[0]
    projected = jnp.dot(
        ffn_input, row_piece.reshape(piece_rows, 2 * unit_count), preferred_element_type=jnp.float32
    )
    hidden = (
        jax.nn.gelu(projected[:, :unit_count], approximate=True) * projected[:, unit_count:]
    ).astype(jnp.bfloat16)
    return (hidden, page_cache)


def solution(mesh):
    return jax.shard_map(
        local,
        mesh=mesh,
        in_specs=(
            P("seq", ("section", "tensor")),
            P(None, ("section", "tensor")),
            P(None, ("section", "tensor")),
            P(("section", "tensor"), None),
            P("seq", None, ("section", "tensor")),
            P(),
            P(),
            P(),
            P(),
            P(),
            P(),
            P("seq"),
        ),
        out_specs=(P("seq", ("section", "tensor")), P("seq", None, ("section", "tensor"))),
        check_vma=False,
    )
```

```python
import jax
import jax.numpy as jnp
from jax import lax
from jax.sharding import PartitionSpec as P

REACH = 16


NORM_EPS = 1e-06
ROPE_BASE = 1000000.0
ROPE_FACTOR = 8.0


def swapped(value, axis, bit):
    mask = 2**bit
    pairs = [(source, source ^ mask) for source in range(lax.axis_size(axis))]
    return lax.ppermute(value, axis, pairs)


def shifted(block, axis, distance):
    devices = range(lax.axis_size(axis))
    route = [(i - distance, i) for i in devices if i - distance in devices]
    return lax.ppermute(block, axis, route)


GROUP = ("section", "tensor")


def group_count():
    return lax.axis_size("section") * lax.axis_size("tensor")


def group_parts(value):
    spread = jnp.broadcast_to(value[None], (group_count(),) + value.shape)
    return lax.all_to_all(spread, GROUP, 0, 0, tiled=True)


def group_gather(block):
    rows, width = block.shape
    parts = group_parts(block)
    return parts.transpose(1, 0, 2).reshape(rows, parts.shape[0] * width)


def group_sum(vector):
    return jnp.sum(group_parts(vector), axis=0)


def rms_norm(values, weights):
    values = values.astype(jnp.float32)
    inverse = lax.rsqrt(jnp.mean(values * values, axis=-1, keepdims=True) + NORM_EPS)
    return values * inverse * weights


def angle_tables(position, head_width):
    halfway = head_width // 2
    exponent = jnp.arange(halfway, dtype=jnp.float32) * (2.0 / head_width)
    frequency = ROPE_BASE ** (-exponent)
    angles = (position.astype(jnp.float32) / ROPE_FACTOR)[:, None] * frequency[None, :]
    return (jnp.cos(angles), jnp.sin(angles))


def rotary(values, cosine_table, sine_table):
    halfway = values.shape[-1] // 2
    lower_half = values[..., :halfway]
    upper_half = values[..., halfway:]
    return jnp.concatenate(
        [
            lower_half * cosine_table - upper_half * sine_table,
            upper_half * cosine_table + lower_half * sine_table,
        ],
        axis=-1,
    )


def local(
    tokens,
    w_query,
    w_keyval,
    w_out,
    w_gateup,
    attn_gain,
    post_gain,
    mlp_gain,
    query_gain,
    key_gain,
    prompt_lengths,
    page_slots,
):
    row_count = tokens.shape[0]
    head_width = w_query.shape[1]
    halfway = head_width // 2
    unit_count = w_gateup.shape[2]
    span_blocks = min(REACH, lax.axis_size("seq") // 2)
    features = group_gather(tokens)
    out_columns = lax.all_to_all(w_out, GROUP, 1, 0, tiled=True)
    first_row = lax.axis_index("seq") * row_count
    prompt_ends = jnp.cumsum(prompt_lengths)
    prompt_starts = prompt_ends - prompt_lengths
    query_index = first_row + jnp.arange(row_count, dtype=jnp.int32)
    query_segment = jnp.sum(
        (prompt_ends[None, :] <= query_index[:, None]).astype(jnp.int32), axis=1
    )
    chosen = query_segment[:, None] == jnp.arange(prompt_ends.shape[0], dtype=jnp.int32)[None, :]
    query_position = query_index - jnp.sum(jnp.where(chosen, prompt_starts[None, :], 0), axis=1)
    cosine_table, sine_table = angle_tables(query_position, head_width)
    normed = rms_norm(features, attn_gain).astype(jnp.bfloat16)
    queries = jnp.dot(normed, w_query, preferred_element_type=jnp.float32)
    queries = rotary(rms_norm(queries, query_gain), cosine_table, sine_table).astype(jnp.bfloat16)
    own_half = jnp.dot(normed, w_keyval, preferred_element_type=jnp.float32).astype(jnp.bfloat16)
    other_half = swapped(own_half, "tensor", 0)
    is_lower = lax.axis_index("tensor") % 2 == 0
    lower_part = jnp.where(is_lower, own_half, other_half)
    upper_part = jnp.where(is_lower, other_half, own_half)
    raw_keys = jnp.concatenate([lower_part[:, :halfway], upper_part[:, :halfway]], axis=1)
    values_full = jnp.concatenate([lower_part[:, halfway:], upper_part[:, halfway:]], axis=1)
    keys_full = rotary(rms_norm(raw_keys, key_gain), cosine_table, sine_table).astype(jnp.bfloat16)
    own_keys = jnp.where(is_lower, keys_full[:, :halfway], keys_full[:, halfway:])
    page_rows = jnp.concatenate([own_keys, own_half[:, halfway:]], axis=1)
    pages_here = page_slots.shape[0]
    page_rows = page_rows.reshape(pages_here, row_count // pages_here, head_width)
    page_cache = jnp.zeros_like(page_rows).at[page_slots].set(page_rows)
    key_block = jnp.stack([keys_full, values_full])
    half_span = span_blocks // 2
    series = key_block[None]
    while series.shape[0] < half_span:
        received = shifted(series, "seq", 2 * series.shape[0])
        series = jnp.concatenate([series, received], axis=0)
    series = jnp.concatenate([series, shifted(key_block, "seq", 2 * half_span)[None]], axis=0)
    partner = swapped(series, "seq", 0)
    parity = lax.axis_index("seq") % 2
    odd = lax.dynamic_slice_in_dim(partner, 1 - parity, half_span, axis=0)
    window_stack = jnp.concatenate([series, odd], axis=0)
    all_keys = window_stack[:, 0].reshape(-1, head_width)
    all_values = window_stack[:, 1].reshape(-1, head_width)
    distances = list(range(0, 2 * half_span + 1, 2)) + list(range(1, 2 * half_span, 2))
    offsets = (jnp.array(distances, dtype=jnp.int32) * row_count)[:, None]
    key_index = (first_row - offsets + jnp.arange(row_count, dtype=jnp.int32)[None, :]).reshape(-1)
    key_segment = jnp.sum((prompt_ends[None, :] <= key_index[:, None]).astype(jnp.int32), axis=1)
    key_segment = jnp.where(key_index >= 0, key_segment, -1)
    allowed = (key_segment[None, :] == query_segment[:, None]) & (
        key_index[None, :] <= query_index[:, None]
    )
    scores = lax.dot_general(
        queries, all_keys, (((1,), (1,)), ((), ())), preferred_element_type=jnp.float32
    ) * head_width ** (-0.5)
    scores = jnp.where(allowed, scores, -jnp.inf)
    row_max = jnp.max(scores, axis=1, keepdims=True)
    exponent_terms = jnp.exp(scores - row_max)
    weights_low = (exponent_terms / jnp.sum(exponent_terms, axis=1, keepdims=True)).astype(
        jnp.bfloat16
    )
    attention_out = jnp.dot(weights_low, all_values, preferred_element_type=jnp.float32).astype(
        jnp.bfloat16
    )
    all_heads = group_gather(attention_out)
    attended = jnp.dot(all_heads, out_columns, preferred_element_type=jnp.float32)
    width = attended.shape[1]
    first_column = lax.axis_index(GROUP) * width
    post_local = lax.dynamic_slice_in_dim(post_gain, first_column, width)
    mlp_local = lax.dynamic_slice_in_dim(mlp_gain, first_column, width)
    model_width = features.shape[1]
    token_rows = tokens.astype(jnp.float32)
    scaled = attended * post_local
    sums = group_sum(
        jnp.stack(
            [
                jnp.sum(attended * attended, axis=1),
                jnp.sum(token_rows * token_rows, axis=1),
                jnp.sum(token_rows * scaled, axis=1),
                jnp.sum(scaled * scaled, axis=1),
            ]
        )
    )
    attended_inverse = lax.rsqrt(sums[0] / model_width + NORM_EPS)
    residual = token_rows + attended * attended_inverse[:, None] * post_local
    residual_square = jnp.maximum(
        sums[1] + 2.0 * attended_inverse * sums[2] + attended_inverse * attended_inverse * sums[3],
        0.0,
    )
    residual_inverse = lax.rsqrt(residual_square / model_width + NORM_EPS)
    ffn_local = (residual * residual_inverse[:, None] * mlp_local).astype(jnp.bfloat16)
    ffn_input = group_gather(ffn_local)
    row_piece = lax.all_gather(
        w_gateup.reshape(w_gateup.shape[0], 2 * unit_count), "seq", axis=0, tiled=True
    )
    projected = jnp.dot(ffn_input, row_piece, preferred_element_type=jnp.float32)
    hidden = (
        jax.nn.gelu(projected[:, :unit_count], approximate=True) * projected[:, unit_count:]
    ).astype(jnp.bfloat16)
    return (hidden, page_cache)


def solution(mesh):
    return jax.shard_map(
        local,
        mesh=mesh,
        in_specs=(
            P("seq", ("section", "tensor")),
            P(None, ("section", "tensor")),
            P(None, ("section", "tensor")),
            P(("section", "tensor"), None),
            P("seq", None, ("section", "tensor")),
            P(),
            P(),
            P(),
            P(),
            P(),
            P(),
            P("seq"),
        ),
        out_specs=(P("seq", ("section", "tensor")), P("seq", None, ("section", "tensor"))),
        check_vma=False,
    )
```

```python
import jax
import jax.numpy as jnp
from jax import lax
from jax.sharding import PartitionSpec as P

REACH = 16


NORM_EPS = 1e-06
ROPE_BASE = 1000000.0
ROPE_FACTOR = 8.0


def swapped(value, axis, bit):
    mask = 2**bit
    pairs = [(source, source ^ mask) for source in range(lax.axis_size(axis))]
    return lax.ppermute(value, axis, pairs)


def shifted(block, axis, distance):
    devices = range(lax.axis_size(axis))
    route = [(i - distance, i) for i in devices if i - distance in devices]
    return lax.ppermute(block, axis, route)


GROUP = ("section", "tensor")


def group_count():
    return lax.axis_size("section") * lax.axis_size("tensor")


def group_parts(value):
    spread = jnp.broadcast_to(value[None], (group_count(),) + value.shape)
    return lax.all_to_all(spread, GROUP, 0, 0, tiled=True)


def group_gather(block):
    rows, width = block.shape
    parts = group_parts(block)
    return parts.transpose(1, 0, 2).reshape(rows, parts.shape[0] * width)


def group_sum(vector):
    return jnp.sum(group_parts(vector), axis=0)


def rms_norm(values, weights):
    values = values.astype(jnp.float32)
    inverse = lax.rsqrt(jnp.mean(values * values, axis=-1, keepdims=True) + NORM_EPS)
    return values * inverse * weights


def angle_tables(position, head_width):
    halfway = head_width // 2
    exponent = jnp.arange(halfway, dtype=jnp.float32) * (2.0 / head_width)
    frequency = ROPE_BASE ** (-exponent)
    angles = (position.astype(jnp.float32) / ROPE_FACTOR)[:, None] * frequency[None, :]
    return (jnp.cos(angles), jnp.sin(angles))


def rotary(values, cosine_table, sine_table):
    halfway = values.shape[-1] // 2
    lower_half = values[..., :halfway]
    upper_half = values[..., halfway:]
    return jnp.concatenate(
        [
            lower_half * cosine_table - upper_half * sine_table,
            upper_half * cosine_table + lower_half * sine_table,
        ],
        axis=-1,
    )


def local(
    tokens,
    w_query,
    w_keyval,
    w_out,
    w_gateup,
    attn_gain,
    post_gain,
    mlp_gain,
    query_gain,
    key_gain,
    prompt_lengths,
    page_slots,
):
    row_count = tokens.shape[0]
    head_width = w_query.shape[1]
    halfway = head_width // 2
    unit_count = w_gateup.shape[2]
    span_blocks = min(REACH, lax.axis_size("seq") // 2)
    features = group_gather(tokens)
    out_columns = lax.all_to_all(w_out, GROUP, 1, 0, tiled=True)
    first_row = lax.axis_index("seq") * row_count
    prompt_ends = jnp.cumsum(prompt_lengths)
    prompt_starts = prompt_ends - prompt_lengths
    query_index = first_row + jnp.arange(row_count, dtype=jnp.int32)
    query_segment = jnp.sum(
        (prompt_ends[None, :] <= query_index[:, None]).astype(jnp.int32), axis=1
    )
    chosen = query_segment[:, None] == jnp.arange(prompt_ends.shape[0], dtype=jnp.int32)[None, :]
    query_position = query_index - jnp.sum(jnp.where(chosen, prompt_starts[None, :], 0), axis=1)
    cosine_table, sine_table = angle_tables(query_position, head_width)
    normed = rms_norm(features, attn_gain).astype(jnp.bfloat16)
    queries = jnp.dot(normed, w_query, preferred_element_type=jnp.float32)
    queries = rotary(rms_norm(queries, query_gain), cosine_table, sine_table).astype(jnp.bfloat16)
    own_half = jnp.dot(normed, w_keyval, preferred_element_type=jnp.float32).astype(jnp.bfloat16)
    other_half = swapped(own_half, "tensor", 0)
    is_lower = lax.axis_index("tensor") % 2 == 0
    lower_part = jnp.where(is_lower, own_half, other_half)
    upper_part = jnp.where(is_lower, other_half, own_half)
    raw_keys = jnp.concatenate([lower_part[:, :halfway], upper_part[:, :halfway]], axis=1)
    values_full = jnp.concatenate([lower_part[:, halfway:], upper_part[:, halfway:]], axis=1)
    keys_full = rotary(rms_norm(raw_keys, key_gain), cosine_table, sine_table).astype(jnp.bfloat16)
    own_keys = jnp.where(is_lower, keys_full[:, :halfway], keys_full[:, halfway:])
    page_rows = jnp.concatenate([own_keys, own_half[:, halfway:]], axis=1)
    pages_here = page_slots.shape[0]
    page_rows = page_rows.reshape(pages_here, row_count // pages_here, head_width)
    page_cache = jnp.zeros_like(page_rows).at[page_slots].set(page_rows)
    key_block = jnp.stack([keys_full, values_full])
    half_span = span_blocks // 2
    series = key_block[None]
    while series.shape[0] < half_span:
        received = shifted(series, "seq", 2 * series.shape[0])
        series = jnp.concatenate([series, received], axis=0)
    series = jnp.concatenate([series, shifted(key_block, "seq", 2 * half_span)[None]], axis=0)
    partner = swapped(series, "seq", 0)
    parity = lax.axis_index("seq") % 2
    lanes = jnp.arange(row_count, dtype=jnp.int32)[None, :]
    own_offsets = jnp.arange(series.shape[0], dtype=jnp.int32)[:, None] * (2 * row_count)
    partner_offsets = own_offsets + (2 * parity - 1) * row_count
    score_scale = head_width ** (-0.5)

    def part_scores(stack, offsets):
        key_index = (first_row - offsets + lanes).reshape(-1)
        key_segment = jnp.sum((prompt_ends[None, :] <= key_index[:, None]).astype(jnp.int32), axis=1)
        key_segment = jnp.where(key_index >= 0, key_segment, -1)
        allowed = (key_segment[None, :] == query_segment[:, None]) & (
            key_index[None, :] <= query_index[:, None]
        )
        keys = stack[:, 0].reshape(-1, head_width)
        scores = lax.dot_general(
            queries, keys, (((1,), (1,)), ((), ())), preferred_element_type=jnp.float32
        ) * score_scale
        return jnp.where(allowed, scores, -jnp.inf)

    own_scores = part_scores(series, own_offsets)
    partner_scores = part_scores(partner, partner_offsets)
    row_max = jnp.maximum(
        jnp.max(own_scores, axis=1, keepdims=True), jnp.max(partner_scores, axis=1, keepdims=True)
    )
    own_terms = jnp.exp(own_scores - row_max)
    partner_terms = jnp.exp(partner_scores - row_max)
    total = jnp.sum(own_terms, axis=1, keepdims=True) + jnp.sum(partner_terms, axis=1, keepdims=True)
    own_probs = (own_terms / total).astype(jnp.bfloat16)
    partner_probs = (partner_terms / total).astype(jnp.bfloat16)
    attention_out = (
        jnp.dot(own_probs, series[:, 1].reshape(-1, head_width), preferred_element_type=jnp.float32)
        + jnp.dot(
            partner_probs, partner[:, 1].reshape(-1, head_width), preferred_element_type=jnp.float32
        )
    ).astype(jnp.bfloat16)
    all_heads = group_gather(attention_out)
    attended = jnp.dot(all_heads, out_columns, preferred_element_type=jnp.float32)
    width = attended.shape[1]
    first_column = lax.axis_index(GROUP) * width
    post_local = lax.dynamic_slice_in_dim(post_gain, first_column, width)
    mlp_local = lax.dynamic_slice_in_dim(mlp_gain, first_column, width)
    model_width = features.shape[1]
    token_rows = tokens.astype(jnp.float32)
    scaled = attended * post_local
    sums = group_sum(
        jnp.stack(
            [
                jnp.sum(attended * attended, axis=1),
                jnp.sum(token_rows * token_rows, axis=1),
                jnp.sum(token_rows * scaled, axis=1),
                jnp.sum(scaled * scaled, axis=1),
            ]
        )
    )
    attended_inverse = lax.rsqrt(sums[0] / model_width + NORM_EPS)
    residual = token_rows + attended * attended_inverse[:, None] * post_local
    residual_square = jnp.maximum(
        sums[1] + 2.0 * attended_inverse * sums[2] + attended_inverse * attended_inverse * sums[3],
        0.0,
    )
    residual_inverse = lax.rsqrt(residual_square / model_width + NORM_EPS)
    ffn_local = (residual * residual_inverse[:, None] * mlp_local).astype(jnp.bfloat16)
    ffn_input = group_gather(ffn_local)
    row_piece = lax.all_gather(
        w_gateup.reshape(w_gateup.shape[0], 2 * unit_count), "seq", axis=0, tiled=True
    )
    projected = jnp.dot(ffn_input, row_piece, preferred_element_type=jnp.float32)
    hidden = (
        jax.nn.gelu(projected[:, :unit_count], approximate=True) * projected[:, unit_count:]
    ).astype(jnp.bfloat16)
    return (hidden, page_cache)


def solution(mesh):
    return jax.shard_map(
        local,
        mesh=mesh,
        in_specs=(
            P("seq", ("section", "tensor")),
            P(None, ("section", "tensor")),
            P(None, ("section", "tensor")),
            P(("section", "tensor"), None),
            P("seq", None, ("section", "tensor")),
            P(),
            P(),
            P(),
            P(),
            P(),
            P(),
            P("seq"),
        ),
        out_specs=(P("seq", ("section", "tensor")), P("seq", None, ("section", "tensor"))),
        check_vma=False,
    )
```

```python
import jax
import jax.numpy as jnp
from jax import lax
from jax.sharding import PartitionSpec as P

REACH = 16


NORM_EPS = 1e-06
ROPE_BASE = 1000000.0
ROPE_FACTOR = 8.0


def swapped(value, axis, bit):
    mask = 2**bit
    pairs = [(source, source ^ mask) for source in range(lax.axis_size(axis))]
    return lax.ppermute(value, axis, pairs)


def shifted(block, axis, distance):
    devices = range(lax.axis_size(axis))
    route = [(i - distance, i) for i in devices if i - distance in devices]
    return lax.ppermute(block, axis, route)


GROUP = ("section", "tensor")


def group_count():
    return lax.axis_size("section") * lax.axis_size("tensor")


def group_parts(value):
    spread = jnp.broadcast_to(value[None], (group_count(),) + value.shape)
    return lax.all_to_all(spread, GROUP, 0, 0, tiled=True)


def group_gather(block):
    rows, width = block.shape
    parts = group_parts(block)
    return parts.transpose(1, 0, 2).reshape(rows, parts.shape[0] * width)


def group_sum(vector):
    return jnp.sum(group_parts(vector), axis=0)


def rms_norm(values, weights):
    values = values.astype(jnp.float32)
    inverse = lax.rsqrt(jnp.mean(values * values, axis=-1, keepdims=True) + NORM_EPS)
    return values * inverse * weights


def angle_tables(position, head_width):
    halfway = head_width // 2
    exponent = jnp.arange(halfway, dtype=jnp.float32) * (2.0 / head_width)
    frequency = ROPE_BASE ** (-exponent)
    angles = (position.astype(jnp.float32) / ROPE_FACTOR)[:, None] * frequency[None, :]
    return (jnp.cos(angles), jnp.sin(angles))


def rotary(values, cosine_table, sine_table):
    halfway = values.shape[-1] // 2
    lower_half = values[..., :halfway]
    upper_half = values[..., halfway:]
    return jnp.concatenate(
        [
            lower_half * cosine_table - upper_half * sine_table,
            upper_half * cosine_table + lower_half * sine_table,
        ],
        axis=-1,
    )


def local(
    tokens,
    w_query,
    w_keyval,
    w_out,
    w_gateup,
    attn_gain,
    post_gain,
    mlp_gain,
    query_gain,
    key_gain,
    prompt_lengths,
    page_slots,
):
    row_count = tokens.shape[0]
    head_width = w_query.shape[1]
    halfway = head_width // 2
    unit_count = w_gateup.shape[2]
    span_blocks = min(REACH, lax.axis_size("seq") // 2)
    features = group_gather(tokens)
    out_columns = lax.all_to_all(w_out, GROUP, 1, 0, tiled=True)
    first_row = lax.axis_index("seq") * row_count
    prompt_ends = jnp.cumsum(prompt_lengths)
    prompt_starts = prompt_ends - prompt_lengths
    query_index = first_row + jnp.arange(row_count, dtype=jnp.int32)
    query_segment = jnp.sum(
        (prompt_ends[None, :] <= query_index[:, None]).astype(jnp.int32), axis=1
    )
    chosen = query_segment[:, None] == jnp.arange(prompt_ends.shape[0], dtype=jnp.int32)[None, :]
    query_position = query_index - jnp.sum(jnp.where(chosen, prompt_starts[None, :], 0), axis=1)
    cosine_table, sine_table = angle_tables(query_position, head_width)
    normed = rms_norm(features, attn_gain).astype(jnp.bfloat16)
    queries = jnp.dot(normed, w_query, preferred_element_type=jnp.float32)
    queries = rotary(rms_norm(queries, query_gain), cosine_table, sine_table).astype(jnp.bfloat16)
    own_half = jnp.dot(normed, w_keyval, preferred_element_type=jnp.float32).astype(jnp.bfloat16)
    other_half = swapped(own_half, "tensor", 0)
    is_lower = lax.axis_index("tensor") % 2 == 0
    lower_part = jnp.where(is_lower, own_half, other_half)
    upper_part = jnp.where(is_lower, other_half, own_half)
    raw_keys = jnp.concatenate([lower_part[:, :halfway], upper_part[:, :halfway]], axis=1)
    values_full = jnp.concatenate([lower_part[:, halfway:], upper_part[:, halfway:]], axis=1)
    keys_full = rotary(rms_norm(raw_keys, key_gain), cosine_table, sine_table).astype(jnp.bfloat16)
    own_keys = jnp.where(is_lower, keys_full[:, :halfway], keys_full[:, halfway:])
    page_rows = jnp.concatenate([own_keys, own_half[:, halfway:]], axis=1)
    pages_here = page_slots.shape[0]
    page_rows = page_rows.reshape(pages_here, row_count // pages_here, head_width)
    page_cache = jnp.zeros_like(page_rows).at[page_slots].set(page_rows)
    key_block = jnp.stack([keys_full, values_full])
    half_span = span_blocks // 2
    near_blocks = half_span // 2
    near = [key_block]
    for step in range(1, near_blocks):
        near.append(shifted(key_block, "seq", 2 * step))
    series = jnp.stack(near)
    received = shifted(series, "seq", 2 * near_blocks)
    series = jnp.concatenate([series, received], axis=0)
    series = jnp.concatenate([series, shifted(key_block, "seq", 2 * half_span)[None]], axis=0)
    partner = swapped(series, "seq", 0)
    parity = lax.axis_index("seq") % 2
    lanes = jnp.arange(row_count, dtype=jnp.int32)[None, :]
    own_offsets = jnp.arange(series.shape[0], dtype=jnp.int32)[:, None] * (2 * row_count)
    partner_offsets = own_offsets + (2 * parity - 1) * row_count
    score_scale = head_width ** (-0.5)

    def part_scores(stack, offsets):
        key_index = (first_row - offsets + lanes).reshape(-1)
        key_segment = jnp.sum((prompt_ends[None, :] <= key_index[:, None]).astype(jnp.int32), axis=1)
        key_segment = jnp.where(key_index >= 0, key_segment, -1)
        allowed = (key_segment[None, :] == query_segment[:, None]) & (
            key_index[None, :] <= query_index[:, None]
        )
        keys = stack[:, 0].reshape(-1, head_width)
        scores = lax.dot_general(
            queries, keys, (((1,), (1,)), ((), ())), preferred_element_type=jnp.float32
        ) * score_scale
        return jnp.where(allowed, scores, -jnp.inf)

    own_scores = part_scores(series, own_offsets)
    partner_scores = part_scores(partner, partner_offsets)
    row_max = jnp.maximum(
        jnp.max(own_scores, axis=1, keepdims=True), jnp.max(partner_scores, axis=1, keepdims=True)
    )
    own_terms = jnp.exp(own_scores - row_max)
    partner_terms = jnp.exp(partner_scores - row_max)
    total = jnp.sum(own_terms, axis=1, keepdims=True) + jnp.sum(partner_terms, axis=1, keepdims=True)
    own_probs = (own_terms / total).astype(jnp.bfloat16)
    partner_probs = (partner_terms / total).astype(jnp.bfloat16)
    attention_out = (
        jnp.dot(own_probs, series[:, 1].reshape(-1, head_width), preferred_element_type=jnp.float32)
        + jnp.dot(
            partner_probs, partner[:, 1].reshape(-1, head_width), preferred_element_type=jnp.float32
        )
    ).astype(jnp.bfloat16)
    all_heads = group_gather(attention_out)
    attended = jnp.dot(all_heads, out_columns, preferred_element_type=jnp.float32)
    width = attended.shape[1]
    first_column = lax.axis_index(GROUP) * width
    post_local = lax.dynamic_slice_in_dim(post_gain, first_column, width)
    mlp_local = lax.dynamic_slice_in_dim(mlp_gain, first_column, width)
    model_width = features.shape[1]
    token_rows = tokens.astype(jnp.float32)
    scaled = attended * post_local
    sums = group_sum(
        jnp.stack(
            [
                jnp.sum(attended * attended, axis=1),
                jnp.sum(token_rows * token_rows, axis=1),
                jnp.sum(token_rows * scaled, axis=1),
                jnp.sum(scaled * scaled, axis=1),
            ]
        )
    )
    attended_inverse = lax.rsqrt(sums[0] / model_width + NORM_EPS)
    residual = token_rows + attended * attended_inverse[:, None] * post_local
    residual_square = jnp.maximum(
        sums[1] + 2.0 * attended_inverse * sums[2] + attended_inverse * attended_inverse * sums[3],
        0.0,
    )
    residual_inverse = lax.rsqrt(residual_square / model_width + NORM_EPS)
    ffn_local = (residual * residual_inverse[:, None] * mlp_local).astype(jnp.bfloat16)
    ffn_input = group_gather(ffn_local)
    row_piece = lax.all_gather(
        w_gateup.reshape(w_gateup.shape[0], 2 * unit_count), "seq", axis=0, tiled=True
    )
    projected = jnp.dot(ffn_input, row_piece, preferred_element_type=jnp.float32)
    hidden = (
        jax.nn.gelu(projected[:, :unit_count], approximate=True) * projected[:, unit_count:]
    ).astype(jnp.bfloat16)
    return (hidden, page_cache)


def solution(mesh):
    return jax.shard_map(
        local,
        mesh=mesh,
        in_specs=(
            P("seq", ("section", "tensor")),
            P(None, ("section", "tensor")),
            P(None, ("section", "tensor")),
            P(("section", "tensor"), None),
            P("seq", None, ("section", "tensor")),
            P(),
            P(),
            P(),
            P(),
            P(),
            P(),
            P("seq"),
        ),
        out_specs=(P("seq", ("section", "tensor")), P("seq", None, ("section", "tensor"))),
        check_vma=False,
    )
```

```python
import jax
import jax.numpy as jnp
from jax import lax
from jax.sharding import PartitionSpec as P

REACH = 16


NORM_EPS = 1e-06
ROPE_BASE = 1000000.0
ROPE_FACTOR = 8.0


def swapped(value, axis, bit):
    mask = 2**bit
    pairs = [(source, source ^ mask) for source in range(lax.axis_size(axis))]
    return lax.ppermute(value, axis, pairs)


def shifted(block, axis, distance):
    devices = range(lax.axis_size(axis))
    route = [(i - distance, i) for i in devices if i - distance in devices]
    return lax.ppermute(block, axis, route)


GROUP = ("section", "tensor")


def group_count():
    return lax.axis_size("section") * lax.axis_size("tensor")


def group_parts(value):
    spread = jnp.broadcast_to(value[None], (group_count(),) + value.shape)
    return lax.all_to_all(spread, GROUP, 0, 0, tiled=True)


def group_gather(block):
    rows, width = block.shape
    parts = group_parts(block)
    return parts.transpose(1, 0, 2).reshape(rows, parts.shape[0] * width)


def rms_norm(values, weights):
    values = values.astype(jnp.float32)
    inverse = lax.rsqrt(jnp.mean(values * values, axis=-1, keepdims=True) + NORM_EPS)
    return values * inverse * weights


def angle_tables(position, head_width):
    halfway = head_width // 2
    exponent = jnp.arange(halfway, dtype=jnp.float32) * (2.0 / head_width)
    frequency = ROPE_BASE ** (-exponent)
    angles = (position.astype(jnp.float32) / ROPE_FACTOR)[:, None] * frequency[None, :]
    return (jnp.cos(angles), jnp.sin(angles))


def rotary(values, cosine_table, sine_table):
    halfway = values.shape[-1] // 2
    lower_half = values[..., :halfway]
    upper_half = values[..., halfway:]
    return jnp.concatenate(
        [
            lower_half * cosine_table - upper_half * sine_table,
            upper_half * cosine_table + lower_half * sine_table,
        ],
        axis=-1,
    )


def local(
    tokens,
    w_query,
    w_keyval,
    w_out,
    w_gateup,
    attn_gain,
    post_gain,
    mlp_gain,
    query_gain,
    key_gain,
    prompt_lengths,
    page_slots,
):
    row_count = tokens.shape[0]
    head_width = w_query.shape[1]
    halfway = head_width // 2
    unit_count = w_gateup.shape[2]
    span_blocks = min(REACH, lax.axis_size("seq") // 2)
    features = group_gather(tokens)
    out_columns = lax.all_to_all(w_out, GROUP, 1, 0, tiled=True)
    first_row = lax.axis_index("seq") * row_count
    prompt_ends = jnp.cumsum(prompt_lengths)
    prompt_starts = prompt_ends - prompt_lengths
    query_index = first_row + jnp.arange(row_count, dtype=jnp.int32)
    query_segment = jnp.sum(
        (prompt_ends[None, :] <= query_index[:, None]).astype(jnp.int32), axis=1
    )
    chosen = query_segment[:, None] == jnp.arange(prompt_ends.shape[0], dtype=jnp.int32)[None, :]
    query_position = query_index - jnp.sum(jnp.where(chosen, prompt_starts[None, :], 0), axis=1)
    cosine_table, sine_table = angle_tables(query_position, head_width)
    normed = rms_norm(features, attn_gain).astype(jnp.bfloat16)
    queries = jnp.dot(normed, w_query, preferred_element_type=jnp.float32)
    queries = rotary(rms_norm(queries, query_gain), cosine_table, sine_table).astype(jnp.bfloat16)
    own_half = jnp.dot(normed, w_keyval, preferred_element_type=jnp.float32).astype(jnp.bfloat16)
    other_half = swapped(own_half, "tensor", 0)
    is_lower = lax.axis_index("tensor") % 2 == 0
    lower_part = jnp.where(is_lower, own_half, other_half)
    upper_part = jnp.where(is_lower, other_half, own_half)
    raw_keys = jnp.concatenate([lower_part[:, :halfway], upper_part[:, :halfway]], axis=1)
    values_full = jnp.concatenate([lower_part[:, halfway:], upper_part[:, halfway:]], axis=1)
    keys_full = rotary(rms_norm(raw_keys, key_gain), cosine_table, sine_table).astype(jnp.bfloat16)
    own_keys = jnp.where(is_lower, keys_full[:, :halfway], keys_full[:, halfway:])
    page_rows = jnp.concatenate([own_keys, own_half[:, halfway:]], axis=1)
    pages_here = page_slots.shape[0]
    page_rows = page_rows.reshape(pages_here, row_count // pages_here, head_width)
    page_cache = jnp.zeros_like(page_rows).at[page_slots].set(page_rows)
    key_block = jnp.stack([keys_full, values_full])
    half_span = span_blocks // 2
    near_blocks = half_span // 2
    near = [key_block]
    for step in range(1, near_blocks):
        near.append(shifted(key_block, "seq", 2 * step))
    series = jnp.stack(near)
    received = shifted(series, "seq", 2 * near_blocks)
    series = jnp.concatenate([series, received], axis=0)
    series = jnp.concatenate([series, shifted(key_block, "seq", 2 * half_span)[None]], axis=0)
    partner = swapped(series, "seq", 0)
    parity = lax.axis_index("seq") % 2
    lanes = jnp.arange(row_count, dtype=jnp.int32)[None, :]
    own_offsets = jnp.arange(series.shape[0], dtype=jnp.int32)[:, None] * (2 * row_count)
    partner_offsets = own_offsets + (2 * parity - 1) * row_count
    score_scale = head_width ** (-0.5)

    def part_scores(stack, offsets):
        key_index = (first_row - offsets + lanes).reshape(-1)
        key_segment = jnp.sum((prompt_ends[None, :] <= key_index[:, None]).astype(jnp.int32), axis=1)
        key_segment = jnp.where(key_index >= 0, key_segment, -1)
        allowed = (key_segment[None, :] == query_segment[:, None]) & (
            key_index[None, :] <= query_index[:, None]
        )
        keys = stack[:, 0].reshape(-1, head_width)
        scores = lax.dot_general(
            queries, keys, (((1,), (1,)), ((), ())), preferred_element_type=jnp.float32
        ) * score_scale
        return jnp.where(allowed, scores, -jnp.inf)

    own_scores = part_scores(series, own_offsets)
    partner_scores = part_scores(partner, partner_offsets)
    row_max = jnp.maximum(
        jnp.max(own_scores, axis=1, keepdims=True), jnp.max(partner_scores, axis=1, keepdims=True)
    )
    own_terms = jnp.exp(own_scores - row_max)
    partner_terms = jnp.exp(partner_scores - row_max)
    total = jnp.sum(own_terms, axis=1, keepdims=True) + jnp.sum(partner_terms, axis=1, keepdims=True)
    own_probs = (own_terms / total).astype(jnp.bfloat16)
    partner_probs = (partner_terms / total).astype(jnp.bfloat16)
    attention_out = (
        jnp.dot(own_probs, series[:, 1].reshape(-1, head_width), preferred_element_type=jnp.float32)
        + jnp.dot(
            partner_probs, partner[:, 1].reshape(-1, head_width), preferred_element_type=jnp.float32
        )
    ).astype(jnp.bfloat16)
    all_heads = group_gather(attention_out)
    attended_local = jnp.dot(all_heads, out_columns, preferred_element_type=jnp.float32)
    attended = group_gather(attended_local.astype(jnp.bfloat16))
    residual = features.astype(jnp.float32) + rms_norm(attended, post_gain)
    ffn_input = rms_norm(residual, mlp_gain).astype(jnp.bfloat16)
    row_piece = lax.all_gather(
        w_gateup.reshape(w_gateup.shape[0], 2 * unit_count), "seq", axis=0, tiled=True
    )
    projected = jnp.dot(ffn_input, row_piece, preferred_element_type=jnp.float32)
    hidden = (
        jax.nn.gelu(projected[:, :unit_count], approximate=True) * projected[:, unit_count:]
    ).astype(jnp.bfloat16)
    return (hidden, page_cache)


def solution(mesh):
    return jax.shard_map(
        local,
        mesh=mesh,
        in_specs=(
            P("seq", ("section", "tensor")),
            P(None, ("section", "tensor")),
            P(None, ("section", "tensor")),
            P(("section", "tensor"), None),
            P("seq", None, ("section", "tensor")),
            P(),
            P(),
            P(),
            P(),
            P(),
            P(),
            P("seq"),
        ),
        out_specs=(P("seq", ("section", "tensor")), P("seq", None, ("section", "tensor"))),
        check_vma=False,
    )
```

```python
import jax
import jax.numpy as jnp
from jax import lax
from jax.sharding import PartitionSpec as P

REACH = 16


NORM_EPS = 1e-06
ROPE_BASE = 1000000.0
ROPE_FACTOR = 8.0


def swapped(value, axis, bit):
    mask = 2**bit
    pairs = [(source, source ^ mask) for source in range(lax.axis_size(axis))]
    return lax.ppermute(value, axis, pairs)


def shifted(block, axis, distance):
    devices = range(lax.axis_size(axis))
    route = [(i - distance, i) for i in devices if i - distance in devices]
    return lax.ppermute(block, axis, route)


GROUP = ("section", "tensor")


def group_count():
    return lax.axis_size("section") * lax.axis_size("tensor")


def group_parts(value):
    spread = jnp.broadcast_to(value[None], (group_count(),) + value.shape)
    return lax.all_to_all(spread, GROUP, 0, 0, tiled=True)


def group_gather(block):
    rows, width = block.shape
    parts = group_parts(block)
    return parts.transpose(1, 0, 2).reshape(rows, parts.shape[0] * width)


def group_sum(vector):
    return jnp.sum(group_parts(vector), axis=0)


def rms_norm(values, weights):
    values = values.astype(jnp.float32)
    inverse = lax.rsqrt(jnp.mean(values * values, axis=-1, keepdims=True) + NORM_EPS)
    return values * inverse * weights


def angle_tables(position, head_width):
    halfway = head_width // 2
    exponent = jnp.arange(halfway, dtype=jnp.float32) * (2.0 / head_width)
    frequency = ROPE_BASE ** (-exponent)
    angles = (position.astype(jnp.float32) / ROPE_FACTOR)[:, None] * frequency[None, :]
    return (jnp.cos(angles), jnp.sin(angles))


def rotary(values, cosine_table, sine_table):
    halfway = values.shape[-1] // 2
    lower_half = values[..., :halfway]
    upper_half = values[..., halfway:]
    return jnp.concatenate(
        [
            lower_half * cosine_table - upper_half * sine_table,
            upper_half * cosine_table + lower_half * sine_table,
        ],
        axis=-1,
    )


def local(
    tokens,
    w_query,
    w_keyval,
    w_out,
    w_gateup,
    attn_gain,
    post_gain,
    mlp_gain,
    query_gain,
    key_gain,
    prompt_lengths,
    page_slots,
):
    row_count = tokens.shape[0]
    head_width = w_query.shape[1]
    halfway = head_width // 2
    unit_count = w_gateup.shape[2]
    span_blocks = min(REACH, lax.axis_size("seq") // 2)
    features = group_gather(tokens)
    out_columns = lax.all_to_all(w_out, GROUP, 1, 0, tiled=True)
    first_row = lax.axis_index("seq") * row_count
    prompt_ends = jnp.cumsum(prompt_lengths)
    prompt_starts = prompt_ends - prompt_lengths
    query_index = first_row + jnp.arange(row_count, dtype=jnp.int32)
    query_segment = jnp.sum(
        (prompt_ends[None, :] <= query_index[:, None]).astype(jnp.int32), axis=1
    )
    chosen = query_segment[:, None] == jnp.arange(prompt_ends.shape[0], dtype=jnp.int32)[None, :]
    query_position = query_index - jnp.sum(jnp.where(chosen, prompt_starts[None, :], 0), axis=1)
    cosine_table, sine_table = angle_tables(query_position, head_width)
    normed = rms_norm(features, attn_gain).astype(jnp.bfloat16)
    queries = jnp.dot(normed, w_query, preferred_element_type=jnp.float32)
    queries = rotary(rms_norm(queries, query_gain), cosine_table, sine_table).astype(jnp.bfloat16)
    own_half = jnp.dot(normed, w_keyval, preferred_element_type=jnp.float32).astype(jnp.bfloat16)
    other_half = swapped(own_half, "tensor", 0)
    is_lower = lax.axis_index("tensor") % 2 == 0
    lower_part = jnp.where(is_lower, own_half, other_half)
    upper_part = jnp.where(is_lower, other_half, own_half)
    raw_keys = jnp.concatenate([lower_part[:, :halfway], upper_part[:, :halfway]], axis=1)
    values_full = jnp.concatenate([lower_part[:, halfway:], upper_part[:, halfway:]], axis=1)
    keys_full = rotary(rms_norm(raw_keys, key_gain), cosine_table, sine_table).astype(jnp.bfloat16)
    own_keys = jnp.where(is_lower, keys_full[:, :halfway], keys_full[:, halfway:])
    page_rows = jnp.concatenate([own_keys, own_half[:, halfway:]], axis=1)
    pages_here = page_slots.shape[0]
    page_rows = page_rows.reshape(pages_here, row_count // pages_here, head_width)
    page_cache = jnp.zeros_like(page_rows).at[page_slots].set(page_rows)
    key_block = jnp.stack([keys_full, values_full])
    half_span = span_blocks // 2
    near_blocks = half_span // 2
    near = [key_block]
    for step in range(1, near_blocks):
        near.append(shifted(key_block, "seq", 2 * step))
    series = jnp.stack(near)
    slow = near_blocks // 2
    early = [i for i in range(near_blocks) if i != slow]
    received_early = shifted(jnp.stack([near[i] for i in early]), "seq", 2 * near_blocks)
    received_late = shifted(near[slow], "seq", 2 * near_blocks)
    far = [received_early[early.index(i)] if i != slow else received_late for i in range(near_blocks)]
    series = jnp.concatenate([series, jnp.stack(far)], axis=0)
    series = jnp.concatenate([series, shifted(key_block, "seq", 2 * half_span)[None]], axis=0)
    partner = swapped(series, "seq", 0)
    parity = lax.axis_index("seq") % 2
    lanes = jnp.arange(row_count, dtype=jnp.int32)[None, :]
    own_offsets = jnp.arange(series.shape[0], dtype=jnp.int32)[:, None] * (2 * row_count)
    partner_offsets = own_offsets + (2 * parity - 1) * row_count
    score_scale = head_width ** (-0.5)

    def part_scores(stack, offsets):
        key_index = (first_row - offsets + lanes).reshape(-1)
        key_segment = jnp.sum((prompt_ends[None, :] <= key_index[:, None]).astype(jnp.int32), axis=1)
        key_segment = jnp.where(key_index >= 0, key_segment, -1)
        allowed = (key_segment[None, :] == query_segment[:, None]) & (
            key_index[None, :] <= query_index[:, None]
        )
        keys = stack[:, 0].reshape(-1, head_width)
        scores = lax.dot_general(
            queries, keys, (((1,), (1,)), ((), ())), preferred_element_type=jnp.float32
        ) * score_scale
        return jnp.where(allowed, scores, -jnp.inf)

    own_scores = part_scores(series, own_offsets)
    partner_scores = part_scores(partner, partner_offsets)
    row_max = jnp.maximum(
        jnp.max(own_scores, axis=1, keepdims=True), jnp.max(partner_scores, axis=1, keepdims=True)
    )
    own_terms = jnp.exp(own_scores - row_max)
    partner_terms = jnp.exp(partner_scores - row_max)
    total = jnp.sum(own_terms, axis=1, keepdims=True) + jnp.sum(partner_terms, axis=1, keepdims=True)
    own_probs = (own_terms / total).astype(jnp.bfloat16)
    partner_probs = (partner_terms / total).astype(jnp.bfloat16)
    attention_out = (
        jnp.dot(own_probs, series[:, 1].reshape(-1, head_width), preferred_element_type=jnp.float32)
        + jnp.dot(
            partner_probs, partner[:, 1].reshape(-1, head_width), preferred_element_type=jnp.float32
        )
    ).astype(jnp.bfloat16)
    all_heads = group_gather(attention_out)
    attended = jnp.dot(all_heads, out_columns, preferred_element_type=jnp.float32)
    width = attended.shape[1]
    first_column = lax.axis_index(GROUP) * width
    post_local = lax.dynamic_slice_in_dim(post_gain, first_column, width)
    mlp_local = lax.dynamic_slice_in_dim(mlp_gain, first_column, width)
    model_width = features.shape[1]
    token_rows = tokens.astype(jnp.float32)
    scaled = attended * post_local
    sums = group_sum(
        jnp.stack(
            [
                jnp.sum(attended * attended, axis=1),
                jnp.sum(token_rows * token_rows, axis=1),
                jnp.sum(token_rows * scaled, axis=1),
                jnp.sum(scaled * scaled, axis=1),
            ]
        )
    )
    attended_inverse = lax.rsqrt(sums[0] / model_width + NORM_EPS)
    residual = token_rows + attended * attended_inverse[:, None] * post_local
    residual_square = jnp.maximum(
        sums[1] + 2.0 * attended_inverse * sums[2] + attended_inverse * attended_inverse * sums[3],
        0.0,
    )
    residual_inverse = lax.rsqrt(residual_square / model_width + NORM_EPS)
    ffn_local = (residual * residual_inverse[:, None] * mlp_local).astype(jnp.bfloat16)
    ffn_input = group_gather(ffn_local)
    row_piece = lax.all_gather(
        w_gateup.reshape(w_gateup.shape[0], 2 * unit_count), "seq", axis=0, tiled=True
    )
    projected = jnp.dot(ffn_input, row_piece, preferred_element_type=jnp.float32)
    hidden = (
        jax.nn.gelu(projected[:, :unit_count], approximate=True) * projected[:, unit_count:]
    ).astype(jnp.bfloat16)
    return (hidden, page_cache)


def solution(mesh):
    return jax.shard_map(
        local,
        mesh=mesh,
        in_specs=(
            P("seq", ("section", "tensor")),
            P(None, ("section", "tensor")),
            P(None, ("section", "tensor")),
            P(("section", "tensor"), None),
            P("seq", None, ("section", "tensor")),
            P(),
            P(),
            P(),
            P(),
            P(),
            P(),
            P("seq"),
        ),
        out_specs=(P("seq", ("section", "tensor")), P("seq", None, ("section", "tensor"))),
        check_vma=False,
    )
```

```python
import jax
import jax.numpy as jnp
from jax import lax
from jax.sharding import PartitionSpec as P

REACH = 16


NORM_EPS = 1e-06
ROPE_BASE = 1000000.0
ROPE_FACTOR = 8.0


def swapped(value, axis, bit):
    mask = 2**bit
    pairs = [(source, source ^ mask) for source in range(lax.axis_size(axis))]
    return lax.ppermute(value, axis, pairs)


def shifted(block, axis, distance):
    devices = range(lax.axis_size(axis))
    route = [(i - distance, i) for i in devices if i - distance in devices]
    return lax.ppermute(block, axis, route)


GROUP = ("section", "tensor")


def group_count():
    return lax.axis_size("section") * lax.axis_size("tensor")


def group_parts(value):
    spread = jnp.broadcast_to(value[None], (group_count(),) + value.shape)
    return lax.all_to_all(spread, GROUP, 0, 0, tiled=True)


def group_gather(block):
    rows, width = block.shape
    parts = group_parts(block)
    return parts.transpose(1, 0, 2).reshape(rows, parts.shape[0] * width)


def group_sum(vector):
    return jnp.sum(group_parts(vector), axis=0)


def rms_norm(values, weights):
    values = values.astype(jnp.float32)
    inverse = lax.rsqrt(jnp.mean(values * values, axis=-1, keepdims=True) + NORM_EPS)
    return values * inverse * weights


def angle_tables(position, head_width):
    halfway = head_width // 2
    exponent = jnp.arange(halfway, dtype=jnp.float32) * (2.0 / head_width)
    frequency = ROPE_BASE ** (-exponent)
    angles = (position.astype(jnp.float32) / ROPE_FACTOR)[:, None] * frequency[None, :]
    return (jnp.cos(angles), jnp.sin(angles))


def rotary(values, cosine_table, sine_table):
    halfway = values.shape[-1] // 2
    lower_half = values[..., :halfway]
    upper_half = values[..., halfway:]
    return jnp.concatenate(
        [
            lower_half * cosine_table - upper_half * sine_table,
            upper_half * cosine_table + lower_half * sine_table,
        ],
        axis=-1,
    )


def local(
    tokens,
    w_query,
    w_keyval,
    w_out,
    w_gateup,
    attn_gain,
    post_gain,
    mlp_gain,
    query_gain,
    key_gain,
    prompt_lengths,
    page_slots,
):
    row_count = tokens.shape[0]
    head_width = w_query.shape[1]
    halfway = head_width // 2
    unit_count = w_gateup.shape[2]
    span_blocks = min(REACH, lax.axis_size("seq") // 2)
    features = group_gather(tokens)
    out_columns = lax.all_to_all(w_out, GROUP, 1, 0, tiled=True)
    first_row = lax.axis_index("seq") * row_count
    prompt_ends = jnp.cumsum(prompt_lengths)
    prompt_starts = prompt_ends - prompt_lengths
    query_index = first_row + jnp.arange(row_count, dtype=jnp.int32)
    query_segment = jnp.sum(
        (prompt_ends[None, :] <= query_index[:, None]).astype(jnp.int32), axis=1
    )
    chosen = query_segment[:, None] == jnp.arange(prompt_ends.shape[0], dtype=jnp.int32)[None, :]
    query_position = query_index - jnp.sum(jnp.where(chosen, prompt_starts[None, :], 0), axis=1)
    cosine_table, sine_table = angle_tables(query_position, head_width)
    normed = rms_norm(features, attn_gain).astype(jnp.bfloat16)
    queries = jnp.dot(normed, w_query, preferred_element_type=jnp.float32)
    queries = rotary(rms_norm(queries, query_gain), cosine_table, sine_table).astype(jnp.bfloat16)
    own_half = jnp.dot(normed, w_keyval, preferred_element_type=jnp.float32).astype(jnp.bfloat16)
    other_half = swapped(own_half, "tensor", 0)
    is_lower = lax.axis_index("tensor") % 2 == 0
    lower_part = jnp.where(is_lower, own_half, other_half)
    upper_part = jnp.where(is_lower, other_half, own_half)
    raw_keys = jnp.concatenate([lower_part[:, :halfway], upper_part[:, :halfway]], axis=1)
    values_full = jnp.concatenate([lower_part[:, halfway:], upper_part[:, halfway:]], axis=1)
    keys_full = rotary(rms_norm(raw_keys, key_gain), cosine_table, sine_table).astype(jnp.bfloat16)
    own_keys = jnp.where(is_lower, keys_full[:, :halfway], keys_full[:, halfway:])
    page_rows = jnp.concatenate([own_keys, own_half[:, halfway:]], axis=1)
    pages_here = page_slots.shape[0]
    page_rows = page_rows.reshape(pages_here, row_count // pages_here, head_width)
    page_cache = jnp.zeros_like(page_rows).at[page_slots].set(page_rows)
    key_block = jnp.stack([keys_full, values_full])
    half_span = span_blocks // 2
    near_blocks = half_span // 2
    near = [key_block]
    for step in range(1, near_blocks):
        near.append(shifted(key_block, "seq", 2 * step))
    series = jnp.stack(near)
    slow = near_blocks // 2
    early = [i for i in range(1, near_blocks) if i != slow]
    received_own = shifted(near[0], "seq", 2 * near_blocks)
    received_early = shifted(jnp.stack([near[i] for i in early]), "seq", 2 * near_blocks)
    received_late = shifted(near[slow], "seq", 2 * near_blocks)
    far = [received_own] + [
        received_early[early.index(i)] if i != slow else received_late for i in range(1, near_blocks)
    ]
    series = jnp.concatenate([series, jnp.stack(far)], axis=0)
    series = jnp.concatenate([series, shifted(key_block, "seq", 2 * half_span)[None]], axis=0)
    partner = swapped(series, "seq", 0)
    parity = lax.axis_index("seq") % 2
    lanes = jnp.arange(row_count, dtype=jnp.int32)[None, :]
    own_offsets = jnp.arange(series.shape[0], dtype=jnp.int32)[:, None] * (2 * row_count)
    partner_offsets = own_offsets + (2 * parity - 1) * row_count
    score_scale = head_width ** (-0.5)

    def part_scores(stack, offsets):
        key_index = (first_row - offsets + lanes).reshape(-1)
        key_segment = jnp.sum((prompt_ends[None, :] <= key_index[:, None]).astype(jnp.int32), axis=1)
        key_segment = jnp.where(key_index >= 0, key_segment, -1)
        allowed = (key_segment[None, :] == query_segment[:, None]) & (
            key_index[None, :] <= query_index[:, None]
        )
        keys = stack[:, 0].reshape(-1, head_width)
        scores = lax.dot_general(
            queries, keys, (((1,), (1,)), ((), ())), preferred_element_type=jnp.float32
        ) * score_scale
        return jnp.where(allowed, scores, -jnp.inf)

    own_scores = part_scores(series, own_offsets)
    partner_scores = part_scores(partner, partner_offsets)
    row_max = jnp.maximum(
        jnp.max(own_scores, axis=1, keepdims=True), jnp.max(partner_scores, axis=1, keepdims=True)
    )
    own_terms = jnp.exp(own_scores - row_max)
    partner_terms = jnp.exp(partner_scores - row_max)
    total = jnp.sum(own_terms, axis=1, keepdims=True) + jnp.sum(partner_terms, axis=1, keepdims=True)
    own_probs = (own_terms / total).astype(jnp.bfloat16)
    partner_probs = (partner_terms / total).astype(jnp.bfloat16)
    attention_out = (
        jnp.dot(own_probs, series[:, 1].reshape(-1, head_width), preferred_element_type=jnp.float32)
        + jnp.dot(
            partner_probs, partner[:, 1].reshape(-1, head_width), preferred_element_type=jnp.float32
        )
    ).astype(jnp.bfloat16)
    all_heads = group_gather(attention_out)
    attended = jnp.dot(all_heads, out_columns, preferred_element_type=jnp.float32)
    width = attended.shape[1]
    first_column = lax.axis_index(GROUP) * width
    post_local = lax.dynamic_slice_in_dim(post_gain, first_column, width)
    mlp_local = lax.dynamic_slice_in_dim(mlp_gain, first_column, width)
    model_width = features.shape[1]
    token_rows = tokens.astype(jnp.float32)
    scaled = attended * post_local
    sums = group_sum(
        jnp.stack(
            [
                jnp.sum(attended * attended, axis=1),
                jnp.sum(token_rows * token_rows, axis=1),
                jnp.sum(token_rows * scaled, axis=1),
                jnp.sum(scaled * scaled, axis=1),
            ]
        )
    )
    attended_inverse = lax.rsqrt(sums[0] / model_width + NORM_EPS)
    residual = token_rows + attended * attended_inverse[:, None] * post_local
    residual_square = jnp.maximum(
        sums[1] + 2.0 * attended_inverse * sums[2] + attended_inverse * attended_inverse * sums[3],
        0.0,
    )
    residual_inverse = lax.rsqrt(residual_square / model_width + NORM_EPS)
    ffn_local = (residual * residual_inverse[:, None] * mlp_local).astype(jnp.bfloat16)
    ffn_input = group_gather(ffn_local)
    row_piece = lax.all_gather(
        w_gateup.reshape(w_gateup.shape[0], 2 * unit_count), "seq", axis=0, tiled=True
    )
    projected = jnp.dot(ffn_input, row_piece, preferred_element_type=jnp.float32)
    hidden = (
        jax.nn.gelu(projected[:, :unit_count], approximate=True) * projected[:, unit_count:]
    ).astype(jnp.bfloat16)
    return (hidden, page_cache)


def solution(mesh):
    return jax.shard_map(
        local,
        mesh=mesh,
        in_specs=(
            P("seq", ("section", "tensor")),
            P(None, ("section", "tensor")),
            P(None, ("section", "tensor")),
            P(("section", "tensor"), None),
            P("seq", None, ("section", "tensor")),
            P(),
            P(),
            P(),
            P(),
            P(),
            P(),
            P("seq"),
        ),
        out_specs=(P("seq", ("section", "tensor")), P("seq", None, ("section", "tensor"))),
        check_vma=False,
    )
```

```python
import jax
import jax.numpy as jnp
from jax import lax
from jax.sharding import PartitionSpec as P

REACH = 16


NORM_EPS = 1e-06
ROPE_BASE = 1000000.0
ROPE_FACTOR = 8.0


def swapped(value, axis, bit):
    mask = 2**bit
    pairs = [(source, source ^ mask) for source in range(lax.axis_size(axis))]
    return lax.ppermute(value, axis, pairs)


def shifted(block, axis, distance):
    devices = range(lax.axis_size(axis))
    route = [(i - distance, i) for i in devices if i - distance in devices]
    return lax.ppermute(block, axis, route)


GROUP = ("section", "tensor")


def group_count():
    return lax.axis_size("section") * lax.axis_size("tensor")


def group_parts(value):
    spread = jnp.broadcast_to(value[None], (group_count(),) + value.shape)
    return lax.all_to_all(spread, GROUP, 0, 0, tiled=True)


def group_gather(block):
    rows, width = block.shape
    parts = group_parts(block)
    return parts.transpose(1, 0, 2).reshape(rows, parts.shape[0] * width)


def group_sum(vector):
    return jnp.sum(group_parts(vector), axis=0)


def rms_norm(values, weights):
    values = values.astype(jnp.float32)
    inverse = lax.rsqrt(jnp.mean(values * values, axis=-1, keepdims=True) + NORM_EPS)
    return values * inverse * weights


def angle_tables(position, head_width):
    halfway = head_width // 2
    exponent = jnp.arange(halfway, dtype=jnp.float32) * (2.0 / head_width)
    frequency = ROPE_BASE ** (-exponent)
    angles = (position.astype(jnp.float32) / ROPE_FACTOR)[:, None] * frequency[None, :]
    return (jnp.cos(angles), jnp.sin(angles))


def rotary(values, cosine_table, sine_table):
    halfway = values.shape[-1] // 2
    lower_half = values[..., :halfway]
    upper_half = values[..., halfway:]
    return jnp.concatenate(
        [
            lower_half * cosine_table - upper_half * sine_table,
            upper_half * cosine_table + lower_half * sine_table,
        ],
        axis=-1,
    )


def local(
    tokens,
    w_query,
    w_keyval,
    w_out,
    w_gateup,
    attn_gain,
    post_gain,
    mlp_gain,
    query_gain,
    key_gain,
    prompt_lengths,
    page_slots,
):
    row_count = tokens.shape[0]
    head_width = w_query.shape[1]
    halfway = head_width // 2
    unit_count = w_gateup.shape[2]
    span_blocks = min(REACH, lax.axis_size("seq") // 2)
    features = group_gather(tokens)
    out_columns = lax.all_to_all(w_out, GROUP, 1, 0, tiled=True)
    first_row = lax.axis_index("seq") * row_count
    prompt_ends = jnp.cumsum(prompt_lengths)
    prompt_starts = prompt_ends - prompt_lengths
    query_index = first_row + jnp.arange(row_count, dtype=jnp.int32)
    query_segment = jnp.sum(
        (prompt_ends[None, :] <= query_index[:, None]).astype(jnp.int32), axis=1
    )
    chosen = query_segment[:, None] == jnp.arange(prompt_ends.shape[0], dtype=jnp.int32)[None, :]
    query_position = query_index - jnp.sum(jnp.where(chosen, prompt_starts[None, :], 0), axis=1)
    cosine_table, sine_table = angle_tables(query_position, head_width)
    normed = rms_norm(features, attn_gain).astype(jnp.bfloat16)
    queries = jnp.dot(normed, w_query, preferred_element_type=jnp.float32)
    queries = rotary(rms_norm(queries, query_gain), cosine_table, sine_table).astype(jnp.bfloat16)
    own_half = jnp.dot(normed, w_keyval, preferred_element_type=jnp.float32).astype(jnp.bfloat16)
    other_half = swapped(own_half, "tensor", 0)
    is_lower = lax.axis_index("tensor") % 2 == 0
    lower_part = jnp.where(is_lower, own_half, other_half)
    upper_part = jnp.where(is_lower, other_half, own_half)
    raw_keys = jnp.concatenate([lower_part[:, :halfway], upper_part[:, :halfway]], axis=1)
    values_full = jnp.concatenate([lower_part[:, halfway:], upper_part[:, halfway:]], axis=1)
    keys_full = rotary(rms_norm(raw_keys, key_gain), cosine_table, sine_table).astype(jnp.bfloat16)
    own_keys = jnp.where(is_lower, keys_full[:, :halfway], keys_full[:, halfway:])
    page_rows = jnp.concatenate([own_keys, own_half[:, halfway:]], axis=1)
    pages_here = page_slots.shape[0]
    page_rows = page_rows.reshape(pages_here, row_count // pages_here, head_width)
    page_cache = jnp.zeros_like(page_rows).at[page_slots].set(page_rows)
    key_block = jnp.stack([keys_full, values_full])
    half_span = span_blocks // 2
    near_blocks = half_span // 2
    near = [key_block]
    for step in range(1, near_blocks):
        near.append(shifted(key_block, "seq", 2 * step))
    series = jnp.stack(near)
    slow = near_blocks // 2
    early = [i for i in range(1, near_blocks) if i != slow]
    received_own = shifted(near[0], "seq", 2 * near_blocks)
    parts = []
    for i in early:
        parts.append(shifted(near[i], "seq", 2 * near_blocks))
    received_early = jnp.stack(parts)
    received_late = shifted(near[slow], "seq", 2 * near_blocks)
    far = [received_own] + [
        received_early[early.index(i)] if i != slow else received_late for i in range(1, near_blocks)
    ]
    series = jnp.concatenate([series, jnp.stack(far)], axis=0)
    series = jnp.concatenate([series, shifted(key_block, "seq", 2 * half_span)[None]], axis=0)
    ready = near_blocks + near_blocks // 2
    partner = jnp.concatenate(
        [swapped(series[:ready], "seq", 0), swapped(series[ready:], "seq", 0)], axis=0
    )
    parity = lax.axis_index("seq") % 2
    lanes = jnp.arange(row_count, dtype=jnp.int32)[None, :]
    own_offsets = jnp.arange(series.shape[0], dtype=jnp.int32)[:, None] * (2 * row_count)
    partner_offsets = own_offsets + (2 * parity - 1) * row_count
    score_scale = head_width ** (-0.5)

    def part_scores(stack, offsets):
        key_index = (first_row - offsets + lanes).reshape(-1)
        key_segment = jnp.sum((prompt_ends[None, :] <= key_index[:, None]).astype(jnp.int32), axis=1)
        key_segment = jnp.where(key_index >= 0, key_segment, -1)
        allowed = (key_segment[None, :] == query_segment[:, None]) & (
            key_index[None, :] <= query_index[:, None]
        )
        keys = stack[:, 0].reshape(-1, head_width)
        scores = lax.dot_general(
            queries, keys, (((1,), (1,)), ((), ())), preferred_element_type=jnp.float32
        ) * score_scale
        return jnp.where(allowed, scores, -jnp.inf)

    own_scores = part_scores(series, own_offsets)
    partner_scores = part_scores(partner, partner_offsets)
    row_max = jnp.maximum(
        jnp.max(own_scores, axis=1, keepdims=True), jnp.max(partner_scores, axis=1, keepdims=True)
    )
    own_terms = jnp.exp(own_scores - row_max)
    partner_terms = jnp.exp(partner_scores - row_max)
    total = jnp.sum(own_terms, axis=1, keepdims=True) + jnp.sum(partner_terms, axis=1, keepdims=True)
    own_probs = (own_terms / total).astype(jnp.bfloat16)
    partner_probs = (partner_terms / total).astype(jnp.bfloat16)
    attention_out = (
        jnp.dot(own_probs, series[:, 1].reshape(-1, head_width), preferred_element_type=jnp.float32)
        + jnp.dot(
            partner_probs, partner[:, 1].reshape(-1, head_width), preferred_element_type=jnp.float32
        )
    ).astype(jnp.bfloat16)
    all_heads = group_gather(attention_out)
    attended = jnp.dot(all_heads, out_columns, preferred_element_type=jnp.float32)
    width = attended.shape[1]
    first_column = lax.axis_index(GROUP) * width
    post_local = lax.dynamic_slice_in_dim(post_gain, first_column, width)
    mlp_local = lax.dynamic_slice_in_dim(mlp_gain, first_column, width)
    model_width = features.shape[1]
    token_rows = tokens.astype(jnp.float32)
    scaled = attended * post_local
    sums = group_sum(
        jnp.stack(
            [
                jnp.sum(attended * attended, axis=1),
                jnp.sum(token_rows * token_rows, axis=1),
                jnp.sum(token_rows * scaled, axis=1),
                jnp.sum(scaled * scaled, axis=1),
            ]
        )
    )
    attended_inverse = lax.rsqrt(sums[0] / model_width + NORM_EPS)
    residual = token_rows + attended * attended_inverse[:, None] * post_local
    residual_square = jnp.maximum(
        sums[1] + 2.0 * attended_inverse * sums[2] + attended_inverse * attended_inverse * sums[3],
        0.0,
    )
    residual_inverse = lax.rsqrt(residual_square / model_width + NORM_EPS)
    ffn_local = (residual * residual_inverse[:, None] * mlp_local).astype(jnp.bfloat16)
    ffn_input = group_gather(ffn_local)
    row_piece = lax.all_gather(
        w_gateup.reshape(w_gateup.shape[0], 2 * unit_count), "seq", axis=0, tiled=True
    )
    projected = jnp.dot(ffn_input, row_piece, preferred_element_type=jnp.float32)
    hidden = (
        jax.nn.gelu(projected[:, :unit_count], approximate=True) * projected[:, unit_count:]
    ).astype(jnp.bfloat16)
    return (hidden, page_cache)


def solution(mesh):
    return jax.shard_map(
        local,
        mesh=mesh,
        in_specs=(
            P("seq", ("section", "tensor")),
            P(None, ("section", "tensor")),
            P(None, ("section", "tensor")),
            P(("section", "tensor"), None),
            P("seq", None, ("section", "tensor")),
            P(),
            P(),
            P(),
            P(),
            P(),
            P(),
            P("seq"),
        ),
        out_specs=(P("seq", ("section", "tensor")), P("seq", None, ("section", "tensor"))),
        check_vma=False,
    )
```
